32 devices in a mesh: front: 8 (over z, x), grp: 4 (over y, core).
Axes of the slice: x: 2, y: 2, z: 4, core: 2. Of those that a mesh axis runs over, the one named last changes fastest.
Arguments:
- front_block: float32 [8, 16384, 1408], P('front', 'grp'), as said below
- child_blocks: float32 [8, 4, 4, 16, 1408], P('front', 'grp'), may hold values from -0.5 to 0.5
- child_rows: int32 [8, 4, 4, 16], P('front', 'grp'), may hold values from 0 to 4095
- child_dest: int32 [8, 4, 4, 1], P('front', 'grp'), may hold values from 0 to 7; in each aligned block of 4 rows (0 to 3, 4 to 7, ..., all dimensions but the last counted through in order) at most 2 rows name the same one
- panel_owner: int32 [8], P('front'), may hold values from 0 to 3
Outputs:
- panel_factor: float32 [8, 16384, 512], P('front', 'grp')
- schur_block: float32 [8, 16384, 896], P('front', 'grp')
The draws below stay inside these ranges and needn't reach their ends.
Inputs may be any that keep to these rules, and one draw needn't show every extreme that they name: `child_dest`: among the 4 blocks of one device no front is named more than 2 times, and in every draw some device names some front exactly 2 times. `front_block`: for every front and row block, the first 512 rows' leading 512 x 512 block has a positive diagonal that dominates; other entries lie within -2.3 to 2.3.
All inputs are finite; a program needn't handle non-finite values.
Results may differ from the reference program's by a relative error of at most 0.0003.
Values sent between devices are 32-bit elements; how exact they have to be, the bound alone decides.
No kernel may reach another device: no remote copies, remote signals or barrier semaphores. Data moves between devices by JAX's collectives and lax.ppermute only.
A program may use at most 128 MiB of HBM per device.

```python
import math
import jax
import jax.numpy as jnp
import numpy as np
from jax import lax

NF = 16384
PB = 512
WIN = 896
KB = 4
BR = 16
CAP = 2
FRONTS = 8
GROUPS = 4
ROWS_DEV = 4096
COLS = 1408


def draw_front_block(key, part):
    key_base = jax.random.fold_in(key, 11)
    key_diag = jax.random.fold_in(key, 23)
    shape = (FRONTS, NF, COLS)
    entries = jax.random.uniform(key_base, shape, jnp.float32, -1.0, 1.0)
    local_row = jnp.arange(NF, dtype=jnp.int32) % ROWS_DEV
    column = jnp.arange(COLS, dtype=jnp.int32)
    is_diag = (local_row[:, None] == column[None, :]) & (local_row[:, None] < PB)
    boost = jax.random.uniform(key_diag, (FRONTS, NF, 1), jnp.float32, 2.0, 3.0) * jnp.sqrt(jnp.float32(PB))
    return entries + jnp.where(is_diag[None, :, :], boost, 0.0)


def touch_ends(array, stream_key, least, largest):
    shape = array.shape
    place = [jax.random.randint(jax.random.fold_in(stream_key, axis), (), 0, shape[axis]) for axis in range(len(shape))]
    array = array.at[tuple(place)].set(least)
    longest = shape.index(max(shape))
    place[longest] = (place[longest] + 1) % shape[longest]
    return array.at[tuple(place)].set(largest)


def steps_of(own_key, extent, pieces, low, largest):
    level = 1.0
    for axis_at, parts in pieces:
        heights = jax.random.uniform(jax.random.fold_in(jax.random.fold_in(own_key, 6), axis_at), (parts,), jnp.float32, low / len(pieces), largest / len(pieces))
        level = level * jnp.repeat(jnp.exp(heights), extent[axis_at] // parts).reshape((-1,) + (1,) * (len(extent) - 1 - axis_at))
    return level


def routed_block(key, own, number, rows, number_of, top, limit, skew):
    sequence = jax.random.permutation(key, number_of)
    packed, ordinary = load_shares(number_of, rows * top, limit, skew, True), load_shares(number_of, rows * top, limit, skew, False)
    places = jnp.arange(number_of)

    def named(lengths, rotation):
        used = int((lengths > 0).sum())
        fixed = max(1, used // 4)
        passed = fixed + (places - fixed + rotation * (used - fixed)) % max(1, number_of - fixed)
        return jnp.zeros((number_of,), jnp.int32).at[sequence[jnp.where(places < fixed, places, passed)]].set(jnp.asarray(lengths, jnp.int32))

    lengths = jnp.where(number % 4 == 0, named(packed, number // 4), named(ordinary, number - number // 4 - 1))
    mixed = jax.random.permutation(jax.random.fold_in(own, 3), number_of)
    giver, taker = mixed[0:number_of // 2 * 2:2], mixed[1:number_of // 2 * 2:2]
    slack = jnp.minimum(lengths[giver] - 1, limit - lengths[taker]) // 2
    slack = jnp.where((giver == sequence[0]) | (taker == sequence[0]) | (lengths[taker] == 0), 0, jnp.maximum(slack, 0))
    passed = jax.random.randint(jax.random.fold_in(own, 4), (number_of // 2,), 0, 1 << 20) % (slack + 1)
    lengths = lengths.at[giver].add(-passed).at[taker].add(passed)
    items = jnp.searchsorted(jnp.cumsum(lengths), jnp.arange(rows * top), side="right").astype(jnp.int32)
    grid = items.reshape(top, rows).T
    grid = grid[jax.random.permutation(jax.random.fold_in(own, 1), rows)]
    rotation = jax.random.randint(jax.random.fold_in(own, 2), (rows, 1), 0, top)
    return jnp.take_along_axis(grid, (jnp.arange(top)[None, :] + rotation) % top, axis=1)


def load_shares(number_of, total, limit, skew, full):
    loads = [(1 << 20) // math.isqrt(grade ** skew) + 1 for grade in range(1, number_of + 1)]
    largest = limit if full else min(limit, max(-(-total // number_of), total * loads[0] // sum(loads)))
    least = 1 if total - largest >= number_of - 1 else 0
    holding, rest = [largest] + [least] * (number_of - 1), total - largest - least * (number_of - 1)
    while rest > 0:
        movable = [i for i in range(1, number_of) if holding[i] < largest] or [i for i in range(1, number_of) if holding[i] < limit]
        whole, remaining = sum([loads[i] for i in movable]), rest
        for i in movable:
            addition = min(limit - holding[i], max(1, remaining * loads[i] // whole), rest)
            holding[i] = holding[i] + addition
            rest = rest - addition
    return np.array(holding)


def setup_inputs(seed: int = 0) -> dict:
    splits = jax.random.split(jax.random.key(seed), 6)
    front_block = draw_front_block(jax.random.fold_in(splits[5], 71), 0)
    child_blocks = jnp.clip(jax.random.uniform(splits[1], (FRONTS, GROUPS, KB, BR, COLS), jnp.float32, -0.5, 0.5) * steps_of(splits[1], (FRONTS, GROUPS, KB, BR, COLS), ((0, 8), (1, 4)), -0.4, 0.0), -0.5, 0.5)
    child_rows = touch_ends(jax.random.randint(splits[2], (FRONTS, GROUPS, KB, BR), 0, ROWS_DEV), jax.random.fold_in(splits[2], 1), 0, ROWS_DEV - 1).astype(jnp.int32)
    child_dest_keys = jax.random.split(jax.random.fold_in(splits[3], 1), FRONTS * GROUPS * KB // KB)
    child_dest_turns = jax.random.permutation(jax.random.fold_in(splits[3], 3), FRONTS * GROUPS * KB // KB)
    child_dest = jax.vmap(lambda own, number: routed_block(jax.random.fold_in(splits[3], 2), own, number, KB, FRONTS, 1, CAP, 2))(child_dest_keys, child_dest_turns).reshape((FRONTS, GROUPS, KB, 1))
    panel_owner = touch_ends(jax.random.randint(splits[4], (FRONTS,), 0, GROUPS), jax.random.fold_in(splits[4], 1), 0, GROUPS - 1).astype(jnp.int32)
    return {"front_block": front_block, "child_blocks": child_blocks, "child_rows": child_rows, "child_dest": child_dest, "panel_owner": panel_owner}


def right_solve(factor, rows):
    return lax.linalg.triangular_solve(factor, rows, left_side=False, lower=True, transpose_a=True)

def factor_front(pair):
    matrix, owner_index = pair
    start_row = (owner_index * ROWS_DEV).astype(jnp.int32)
    zero_index = jnp.zeros((), jnp.int32)
    pivot_block = lax.dynamic_slice(matrix, (start_row, zero_index), (PB, PB))
    symmetric = 0.5 * (pivot_block + pivot_block.T)
    pivot_factor = jnp.linalg.cholesky(symmetric)
    solved = right_solve(pivot_factor, matrix[:, :PB])
    window = lax.dynamic_slice(solved, (start_row + PB, zero_index), (WIN, PB))
    schur_part = matrix[:, PB:] - jnp.dot(solved, window.T, precision=lax.Precision.HIGHEST)
    panel_rows = lax.dynamic_update_slice(solved, pivot_factor, (start_row, zero_index))
    return (panel_rows, schur_part)

def reference(front_block, child_blocks, child_rows, child_dest, panel_owner):
    flattened = front_block.reshape(FRONTS * NF, COLS)
    group_base = (jnp.arange(GROUPS, dtype=jnp.int32) * ROWS_DEV)[None, :, None, None]
    target = child_dest[..., 0][..., None] * NF + group_base + child_rows
    flattened = flattened.at[target.reshape(-1)].add(child_blocks.reshape(-1, COLS))
    assembled = flattened.reshape(FRONTS, NF, COLS)
    panel_factor, schur_block = lax.map(factor_front, (assembled, panel_owner))
    return (panel_factor, schur_block)
```

```python
import jax
import jax.numpy as jnp
from jax import lax
from jax.sharding import PartitionSpec as P

PB = 512
CAP = 2
BLK = 128
EXACT = lax.Precision.HIGHEST
FAST = lax.Precision.HIGH


def pack_slots(values, slot_index, front_count):
    empty = jnp.zeros((front_count * CAP,) + values.shape[1:], values.dtype)
    filled = empty.at[slot_index].set(values)
    return filled.reshape((front_count, CAP) + values.shape[1:])


def pairs(size, bit):
    return [(d, d ^ bit) for d in range(size)]


def broadcast_from(x, owner, axis):
    size = lax.axis_size(axis)
    me = lax.axis_index(axis)
    got = lax.ppermute(x, axis, pairs(size, 1))
    x = jnp.where(me == owner, x, got)
    half_rows = x.shape[0] // 2
    core = me % 2
    half = jnp.where(core == 0, x[:half_rows], x[half_rows:])
    bit = 2
    while bit < size:
        got = lax.ppermute(half, axis, pairs(size, bit))
        half = jnp.where(me // bit == owner // bit, half, got)
        bit *= 2
    other = lax.ppermute(half, axis, pairs(size, 1))
    return jnp.where(
        core == 0,
        jnp.concatenate([half, other], axis=0),
        jnp.concatenate([other, half], axis=0),
    )


def tri_inverse(factor):
    eye = jnp.eye(factor.shape[0], dtype=factor.dtype)
    return lax.linalg.triangular_solve(factor, eye, left_side=True, lower=True)


def cholesky_and_inverse(sym):
    n = sym.shape[0]
    nb = n // BLK
    blk = [[None] * nb for _ in range(nb)]
    inv_diag = []
    for k in range(nb):
        akk = sym[k * BLK:(k + 1) * BLK, k * BLK:(k + 1) * BLK]
        for j in range(k):
            akk = akk - jnp.dot(blk[k][j], blk[k][j].T, precision=EXACT)
        lkk = jnp.linalg.cholesky(akk)
        ikk = tri_inverse(lkk)
        blk[k][k] = lkk
        inv_diag.append(ikk)
        if k + 1 < nb:
            rest = sym[(k + 1) * BLK:, k * BLK:(k + 1) * BLK]
            for j in range(k):
                below = jnp.concatenate([blk[i][j] for i in range(k + 1, nb)], axis=0)
                rest = rest - jnp.dot(below, blk[k][j].T, precision=EXACT)
            panel = jnp.dot(rest, ikk.T, precision=EXACT)
            for i in range(k + 1, nb):
                blk[i][k] = panel[(i - k - 1) * BLK:(i - k) * BLK]
    inv = [[None] * nb for _ in range(nb)]
    for i in range(nb):
        inv[i][i] = inv_diag[i]
        for j in range(i - 1, -1, -1):
            acc = jnp.dot(blk[i][j], inv[j][j], precision=EXACT)
            for k in range(j + 1, i):
                acc = acc + jnp.dot(blk[i][k], inv[k][j], precision=EXACT)
            inv[i][j] = -jnp.dot(inv_diag[i], acc, precision=EXACT)
    zero = jnp.zeros((BLK, BLK), sym.dtype)

    def join(parts):
        return jnp.concatenate(
            [jnp.concatenate([parts[i][j] if j <= i else zero for j in range(nb)], axis=1) for i in range(nb)],
            axis=0,
        )

    return join(blk), join(inv)


def local(front_block, child_blocks, child_rows, child_dest, panel_owner):
    local_rows = front_block[0]
    front_count = lax.axis_size("front")
    blocks = child_blocks[0, 0]
    row_lists = child_rows[0, 0]
    target_front = child_dest[0, 0, :, 0]
    block_count = target_front.shape[0]
    position = jnp.arange(block_count, dtype=jnp.int32)
    same_front = target_front[:, None] == target_front[None, :]
    earlier = position[None, :] < position[:, None]
    slot_index = target_front * CAP + jnp.sum((same_front & earlier).astype(jnp.int32), axis=1)
    send_rows = pack_slots(row_lists, slot_index, front_count)
    send_panel = pack_slots(blocks[:, :, :PB], slot_index, front_count)
    got_panel = lax.all_to_all(send_panel, "front", split_axis=0, concat_axis=0, tiled=True)
    got_rows = lax.all_to_all(send_rows, "front", split_axis=0, concat_axis=0, tiled=True)
    flat_rows = got_rows.reshape(-1)
    panel_part = local_rows[:, :PB].at[flat_rows].add(got_panel.reshape(-1, PB))
    send_trail = pack_slots(blocks[:, :, PB:], slot_index, front_count)
    trailing_rows = lax.all_to_all(send_trail, "front", split_axis=0, concat_axis=0, tiled=True)
    win_cols = local_rows.shape[1] - PB
    owner_index = panel_owner[0]
    is_owner = lax.axis_index("grp") == owner_index

    pivot_block = broadcast_from(panel_part[:PB], owner_index, "grp")
    window_rows = broadcast_from(panel_part[PB:PB + win_cols], owner_index, "grp")
    symmetric = 0.5 * (pivot_block + pivot_block.T)
    pivot_factor, factor_inverse = cholesky_and_inverse(symmetric)
    solved = jnp.dot(panel_part, factor_inverse.T, precision=FAST)
    window = jnp.dot(window_rows, factor_inverse.T, precision=FAST)
    schur_part = local_rows[:, PB:] - jnp.dot(solved, window.T, precision=FAST)
    schur_part = schur_part.at[flat_rows].add(trailing_rows.reshape(-1, win_cols))
    top_rows = jnp.where(is_owner, pivot_factor, solved[:PB])
    panel_rows = jnp.concatenate([top_rows, solved[PB:]], axis=0)
    return (panel_rows[None], schur_part[None])


def solution(mesh):
    placed = (
        P("front", "grp", None),
        P("front", "grp", None, None, None),
        P("front", "grp", None, None),
        P("front", "grp", None, None),
        P("front"),
    )
    return jax.shard_map(
        local,
        mesh=mesh,
        in_specs=placed,
        out_specs=(P("front", "grp", None), P("front", "grp", None)),
        check_vma=False,
    )
```

```python
import jax
import jax.numpy as jnp
from jax import lax
from jax.experimental import pallas as pl
from jax.experimental.pallas import tpu as pltpu
from jax.sharding import PartitionSpec as P

PB = 512
CAP = 2
BLK = 128
EXACT = lax.Precision.HIGHEST
FAST = lax.Precision.HIGH


def pack_slots(values, slot_index, front_count):
    empty = jnp.zeros((front_count * CAP,) + values.shape[1:], values.dtype)
    filled = empty.at[slot_index].set(values)
    return filled.reshape((front_count, CAP) + values.shape[1:])


def pairs(size, bit):
    return [(d, d ^ bit) for d in range(size)]


def broadcast_from(x, owner, axis):
    size = lax.axis_size(axis)
    me = lax.axis_index(axis)
    got = lax.ppermute(x, axis, pairs(size, 1))
    x = jnp.where(me == owner, x, got)
    half_rows = x.shape[0] // 2
    core = me % 2
    half = jnp.where(core == 0, x[:half_rows], x[half_rows:])
    bit = 2
    while bit < size:
        got = lax.ppermute(half, axis, pairs(size, bit))
        half = jnp.where(me // bit == owner // bit, half, got)
        bit *= 2
    other = lax.ppermute(half, axis, pairs(size, 1))
    return jnp.where(
        core == 0,
        jnp.concatenate([half, other], axis=0),
        jnp.concatenate([other, half], axis=0),
    )


def _mm(a, b):
    return jnp.dot(a, b, precision=EXACT, preferred_element_type=jnp.float32)


def _mm_t(a, b):
    return lax.dot_general(a, b, (((1,), (1,)), ((), ())), precision=EXACT, preferred_element_type=jnp.float32)


def _factor_kernel(s_ref, l_ref, inv_ref, w_ref, d_ref, dt_ref, di_ref):
    n = s_ref.shape[0]
    nb = n // BLK
    w_ref[...] = s_ref[...]
    l_ref[...] = jnp.zeros_like(l_ref)
    inv_ref[...] = jnp.zeros_like(inv_ref)
    sub = lax.broadcasted_iota(jnp.int32, (BLK, BLK), 0)
    lane = lax.broadcasted_iota(jnp.int32, (BLK, BLK), 1)
    lane1 = lax.broadcasted_iota(jnp.int32, (1, BLK), 1)
    sub1 = lax.broadcasted_iota(jnp.int32, (BLK, 1), 0)
    eye = jnp.where(sub == lane, 1.0, 0.0).astype(jnp.float32)

    def step(j, carry):
        row = d_ref[pl.ds(j, 1), :]
        d = jnp.sum(jnp.where(lane1 == j, row, 0.0), axis=1, keepdims=True)
        s = lax.rsqrt(d)
        c = jnp.where(lane1 >= j, row * s, 0.0)
        wv = d_ref[...]
        col = jnp.sum(jnp.where(lane == j, wv, 0.0), axis=1, keepdims=True)
        ccol = jnp.where(sub1 >= j, col * s, 0.0)
        d_ref[...] = wv - ccol * c
        dt_ref[pl.ds(j, 1), :] = c
        xrow = di_ref[pl.ds(j, 1), :] * s
        di_ref[...] = di_ref[...] - jnp.where(sub1 > j, ccol, 0.0) * xrow
        di_ref[pl.ds(j, 1), :] = xrow
        return carry

    inv_diag = []
    for k in range(nb):
        lo, hi = k * BLK, (k + 1) * BLK
        d_ref[...] = w_ref[lo:hi, lo:hi]
        di_ref[...] = eye
        lax.fori_loop(0, BLK, step, 0)
        lkk = dt_ref[...].T
        ikk = di_ref[...]
        l_ref[lo:hi, lo:hi] = lkk
        inv_ref[lo:hi, lo:hi] = ikk
        inv_diag.append(ikk)
        if k + 1 < nb:
            panel = _mm_t(w_ref[hi:, lo:hi], ikk)
            l_ref[hi:, lo:hi] = panel
            w_ref[hi:, hi:] = w_ref[hi:, hi:] - _mm_t(panel, panel)
    for i in range(nb):
        for j in range(i - 1, -1, -1):
            acc = _mm(l_ref[i * BLK:(i + 1) * BLK, j * BLK:i * BLK], inv_ref[j * BLK:i * BLK, j * BLK:(j + 1) * BLK])
            inv_ref[i * BLK:(i + 1) * BLK, j * BLK:(j + 1) * BLK] = -_mm(inv_diag[i], acc)


def factor_and_inverse(sym):
    n = sym.shape[0]
    return pl.pallas_call(
        _factor_kernel,
        out_shape=(jax.ShapeDtypeStruct((n, n), jnp.float32), jax.ShapeDtypeStruct((n, n), jnp.float32)),
        in_specs=[pl.BlockSpec(memory_space=pltpu.VMEM)],
        out_specs=(pl.BlockSpec(memory_space=pltpu.VMEM), pl.BlockSpec(memory_space=pltpu.VMEM)),
        scratch_shapes=[pltpu.VMEM((n, n), jnp.float32)] + [pltpu.VMEM((BLK, BLK), jnp.float32)] * 3,
    )(sym)


def local(front_block, child_blocks, child_rows, child_dest, panel_owner):
    local_rows = front_block[0]
    front_count = lax.axis_size("front")
    blocks = child_blocks[0, 0]
    row_lists = child_rows[0, 0]
    target_front = child_dest[0, 0, :, 0]
    block_count = target_front.shape[0]
    position = jnp.arange(block_count, dtype=jnp.int32)
    same_front = target_front[:, None] == target_front[None, :]
    earlier = position[None, :] < position[:, None]
    slot_index = target_front * CAP + jnp.sum((same_front & earlier).astype(jnp.int32), axis=1)
    send_rows = pack_slots(row_lists, slot_index, front_count)
    send_panel = pack_slots(blocks[:, :, :PB], slot_index, front_count)
    got_panel = lax.all_to_all(send_panel, "front", split_axis=0, concat_axis=0, tiled=True)
    got_rows = lax.all_to_all(send_rows, "front", split_axis=0, concat_axis=0, tiled=True)
    flat_rows = got_rows.reshape(-1)
    panel_part = local_rows[:, :PB].at[flat_rows].add(got_panel.reshape(-1, PB))
    send_trail = pack_slots(blocks[:, :, PB:], slot_index, front_count)
    trailing_rows = lax.all_to_all(send_trail, "front", split_axis=0, concat_axis=0, tiled=True)
    win_cols = local_rows.shape[1] - PB
    owner_index = panel_owner[0]
    is_owner = lax.axis_index("grp") == owner_index

    pivot_block = broadcast_from(panel_part[:PB], owner_index, "grp")
    window_rows = broadcast_from(panel_part[PB:PB + win_cols], owner_index, "grp")
    symmetric = 0.5 * (pivot_block + pivot_block.T)
    pivot_factor, factor_inverse = factor_and_inverse(symmetric)
    solved = jnp.dot(panel_part, factor_inverse.T, precision=FAST)
    window = jnp.dot(window_rows, factor_inverse.T, precision=FAST)
    schur_part = local_rows[:, PB:] - jnp.dot(solved, window.T, precision=FAST)
    schur_part = schur_part.at[flat_rows].add(trailing_rows.reshape(-1, win_cols))
    top_rows = jnp.where(is_owner, pivot_factor, solved[:PB])
    panel_rows = jnp.concatenate([top_rows, solved[PB:]], axis=0)
    return (panel_rows[None], schur_part[None])


def solution(mesh):
    placed = (
        P("front", "grp", None),
        P("front", "grp", None, None, None),
        P("front", "grp", None, None),
        P("front", "grp", None, None),
        P("front"),
    )
    return jax.shard_map(
        local,
        mesh=mesh,
        in_specs=placed,
        out_specs=(P("front", "grp", None), P("front", "grp", None)),
        check_vma=False,
    )
```

```python
import jax
import jax.numpy as jnp
from jax import lax
from jax.experimental import pallas as pl
from jax.experimental.pallas import tpu as pltpu
from jax.sharding import PartitionSpec as P

PB = 512
CAP = 2
BLK = 128
EXACT = lax.Precision.HIGHEST
FAST = lax.Precision.HIGH


def pack_slots(values, slot_index, front_count):
    empty = jnp.zeros((front_count * CAP,) + values.shape[1:], values.dtype)
    filled = empty.at[slot_index].set(values)
    return filled.reshape((front_count, CAP) + values.shape[1:])


def pairs(size, bit):
    return [(d, d ^ bit) for d in range(size)]


def broadcast_from(x, owner, axis):
    size = lax.axis_size(axis)
    me = lax.axis_index(axis)
    got = lax.ppermute(x, axis, pairs(size, 1))
    x = jnp.where(me == owner, x, got)
    half_rows = x.shape[0] // 2
    core = me % 2
    half = jnp.where(core == 0, x[:half_rows], x[half_rows:])
    bit = 2
    while bit < size:
        got = lax.ppermute(half, axis, pairs(size, bit))
        half = jnp.where(me // bit == owner // bit, half, got)
        bit *= 2
    other = lax.ppermute(half, axis, pairs(size, 1))
    return jnp.where(
        core == 0,
        jnp.concatenate([half, other], axis=0),
        jnp.concatenate([other, half], axis=0),
    )


def _mm(a, b):
    return jnp.dot(a, b, precision=EXACT, preferred_element_type=jnp.float32)


def _mm_t(a, b):
    return lax.dot_general(a, b, (((1,), (1,)), ((), ())), precision=EXACT, preferred_element_type=jnp.float32)


def _factor_kernel(s_ref, l_ref, inv_ref, w_ref, d_ref, dt_ref, di_ref):
    n = s_ref.shape[0]
    nb = n // BLK
    w_ref[...] = s_ref[...]
    l_ref[...] = jnp.zeros_like(l_ref)
    inv_ref[...] = jnp.zeros_like(inv_ref)
    sub = lax.broadcasted_iota(jnp.int32, (BLK, BLK), 0)
    lane = lax.broadcasted_iota(jnp.int32, (BLK, BLK), 1)
    lane1 = lax.broadcasted_iota(jnp.int32, (1, BLK), 1)
    sub1 = lax.broadcasted_iota(jnp.int32, (BLK, 1), 0)
    eye = jnp.where(sub == lane, 1.0, 0.0).astype(jnp.float32)

    def step(j, carry):
        row = d_ref[pl.ds(j, 1), :]
        d = jnp.sum(jnp.where(lane1 == j, row, 0.0), axis=1, keepdims=True)
        s = lax.rsqrt(d)
        c = jnp.where(lane1 >= j, row * s, 0.0)
        wv = d_ref[...]
        col = jnp.sum(jnp.where(lane == j, wv, 0.0), axis=1, keepdims=True)
        ccol = jnp.where(sub1 >= j, col * s, 0.0)
        d_ref[...] = wv - ccol * c
        dt_ref[pl.ds(j, 1), :] = c
        xrow = di_ref[pl.ds(j, 1), :] * s
        di_ref[...] = di_ref[...] - jnp.where(sub1 > j, ccol, 0.0) * xrow
        di_ref[pl.ds(j, 1), :] = xrow
        return carry

    inv_diag = []
    for k in range(nb):
        lo, hi = k * BLK, (k + 1) * BLK
        d_ref[...] = w_ref[lo:hi, lo:hi]
        di_ref[...] = eye
        lax.fori_loop(0, BLK, step, 0)
        lkk = dt_ref[...].T
        ikk = di_ref[...]
        l_ref[lo:hi, lo:hi] = lkk
        inv_ref[lo:hi, lo:hi] = ikk
        inv_diag.append(ikk)
        if k + 1 < nb:
            panel = _mm_t(w_ref[hi:, lo:hi], ikk)
            l_ref[hi:, lo:hi] = panel
            w_ref[hi:, hi:] = w_ref[hi:, hi:] - _mm_t(panel, panel)
    for i in range(nb):
        for j in range(i - 1, -1, -1):
            acc = _mm(l_ref[i * BLK:(i + 1) * BLK, j * BLK:i * BLK], inv_ref[j * BLK:i * BLK, j * BLK:(j + 1) * BLK])
            inv_ref[i * BLK:(i + 1) * BLK, j * BLK:(j + 1) * BLK] = -_mm(inv_diag[i], acc)


def factor_and_inverse(sym):
    n = sym.shape[0]
    return pl.pallas_call(
        _factor_kernel,
        out_shape=(jax.ShapeDtypeStruct((n, n), jnp.float32), jax.ShapeDtypeStruct((n, n), jnp.float32)),
        in_specs=[pl.BlockSpec(memory_space=pltpu.VMEM)],
        out_specs=(pl.BlockSpec(memory_space=pltpu.VMEM), pl.BlockSpec(memory_space=pltpu.VMEM)),
        scratch_shapes=[pltpu.VMEM((n, n), jnp.float32)] + [pltpu.VMEM((BLK, BLK), jnp.float32)] * 3,
    )(sym)


def local(front_block, child_blocks, child_rows, child_dest, panel_owner):
    local_rows = front_block[0]
    row_count, col_count = local_rows.shape
    win_cols = col_count - PB
    front_count = lax.axis_size("front")
    blocks = child_blocks[0, 0]
    row_lists = child_rows[0, 0]
    target_front = child_dest[0, 0, :, 0]
    block_count = target_front.shape[0]
    position = jnp.arange(block_count, dtype=jnp.int32)
    same_front = target_front[:, None] == target_front[None, :]
    earlier = position[None, :] < position[:, None]
    slot_index = target_front * CAP + jnp.sum((same_front & earlier).astype(jnp.int32), axis=1)
    send_rows = pack_slots(row_lists, slot_index, front_count)
    send_blocks = pack_slots(blocks, slot_index, front_count)
    got_rows = lax.all_to_all(send_rows, "front", split_axis=0, concat_axis=0, tiled=True)
    got_blocks = lax.all_to_all(send_blocks, "front", split_axis=0, concat_axis=0, tiled=True)
    flat_rows = got_rows.reshape(-1)
    got_blocks = got_blocks.reshape(-1, col_count)
    got_panel = got_blocks[:, :PB]
    got_trail = got_blocks[:, PB:]
    owner_index = panel_owner[0]
    is_owner = lax.axis_index("grp") == owner_index

    top_count = PB + win_cols
    top_hits = (jnp.arange(top_count, dtype=jnp.int32)[:, None] == flat_rows[None, :]).astype(jnp.float32)
    top_rows = local_rows[:top_count, :PB] + jnp.dot(top_hits, got_panel, precision=EXACT)
    pivot_block = broadcast_from(top_rows[:PB], owner_index, "grp")
    window_rows = broadcast_from(top_rows[PB:], owner_index, "grp")
    symmetric = 0.5 * (pivot_block + pivot_block.T)
    pivot_factor, factor_inverse = factor_and_inverse(symmetric)

    hits = (jnp.arange(row_count, dtype=jnp.int32)[:, None] == flat_rows[None, :]).astype(jnp.float32)
    child_solved = jnp.dot(got_panel, factor_inverse.T, precision=EXACT)
    solved = jnp.dot(local_rows[:, :PB], factor_inverse.T, precision=FAST) + jnp.dot(hits, child_solved, precision=FAST)
    window = jnp.dot(window_rows, factor_inverse.T, precision=FAST)
    schur_part = (
        local_rows[:, PB:]
        - jnp.dot(solved, window.T, precision=FAST)
        + jnp.dot(hits, got_trail, precision=FAST)
    )
    head = jnp.where(is_owner, pivot_factor, solved[:PB])
    panel_rows = lax.dynamic_update_slice(solved, head, (0, 0))
    return (panel_rows[None], schur_part[None])


def solution(mesh):
    placed = (
        P("front", "grp", None),
        P("front", "grp", None, None, None),
        P("front", "grp", None, None),
        P("front", "grp", None, None),
        P("front"),
    )
    return jax.shard_map(
        local,
        mesh=mesh,
        in_specs=placed,
        out_specs=(P("front", "grp", None), P("front", "grp", None)),
        check_vma=False,
    )
```

```python
import jax
import jax.numpy as jnp
from jax import lax
from jax.experimental import pallas as pl
from jax.experimental.pallas import tpu as pltpu
from jax.sharding import PartitionSpec as P

PB = 512
CAP = 2
BLK = 128
EXACT = lax.Precision.HIGHEST
FAST = lax.Precision.HIGH


def pack_slots(values, slot_index, front_count):
    empty = jnp.zeros((front_count * CAP,) + values.shape[1:], values.dtype)
    filled = empty.at[slot_index].set(values)
    return filled.reshape((front_count, CAP) + values.shape[1:])


def pairs(size, bit):
    return [(d, d ^ bit) for d in range(size)]


def broadcast_from(x, owner, axis):
    size = lax.axis_size(axis)
    me = lax.axis_index(axis)
    got = lax.ppermute(x, axis, pairs(size, 1))
    x = jnp.where(me == owner, x, got)
    half_rows = x.shape[0] // 2
    core = me % 2
    half = jnp.where(core == 0, x[:half_rows], x[half_rows:])
    bit = 2
    while bit < size:
        got = lax.ppermute(half, axis, pairs(size, bit))
        half = jnp.where(me // bit == owner // bit, half, got)
        bit *= 2
    other = lax.ppermute(half, axis, pairs(size, 1))
    return jnp.where(
        core == 0,
        jnp.concatenate([half, other], axis=0),
        jnp.concatenate([other, half], axis=0),
    )


def _mm(a, b):
    return jnp.dot(a, b, precision=EXACT, preferred_element_type=jnp.float32)


def _mm_t(a, b):
    return lax.dot_general(a, b, (((1,), (1,)), ((), ())), precision=EXACT, preferred_element_type=jnp.float32)


def _factor_kernel(s_ref, l_ref, inv_ref, w_ref, d_ref, dt_ref, di_ref):
    n = s_ref.shape[0]
    nb = n // BLK
    w_ref[...] = s_ref[...]
    l_ref[...] = jnp.zeros_like(l_ref)
    inv_ref[...] = jnp.zeros_like(inv_ref)
    sub = lax.broadcasted_iota(jnp.int32, (BLK, BLK), 0)
    lane = lax.broadcasted_iota(jnp.int32, (BLK, BLK), 1)
    lane1 = lax.broadcasted_iota(jnp.int32, (1, BLK), 1)
    sub1 = lax.broadcasted_iota(jnp.int32, (BLK, 1), 0)
    eye = jnp.where(sub == lane, 1.0, 0.0).astype(jnp.float32)

    def step(j, carry):
        row = d_ref[pl.ds(j, 1), :]
        d = jnp.sum(jnp.where(lane1 == j, row, 0.0), axis=1, keepdims=True)
        s = lax.rsqrt(d)
        c = jnp.where(lane1 >= j, row * s, 0.0)
        wv = d_ref[...]
        col = jnp.sum(jnp.where(lane == j, wv, 0.0), axis=1, keepdims=True)
        ccol = jnp.where(sub1 >= j, col * s, 0.0)
        d_ref[...] = wv - ccol * c
        dt_ref[pl.ds(j, 1), :] = c
        xrow = di_ref[pl.ds(j, 1), :] * s
        di_ref[...] = di_ref[...] - jnp.where(sub1 > j, ccol, 0.0) * xrow
        di_ref[pl.ds(j, 1), :] = xrow
        return carry

    inv_diag = []
    for k in range(nb):
        lo, hi = k * BLK, (k + 1) * BLK
        d_ref[...] = w_ref[lo:hi, lo:hi]
        di_ref[...] = eye
        lax.fori_loop(0, BLK, step, 0)
        lkk = dt_ref[...].T
        ikk = di_ref[...]
        l_ref[lo:hi, lo:hi] = lkk
        inv_ref[lo:hi, lo:hi] = ikk
        inv_diag.append(ikk)
        if k + 1 < nb:
            panel = _mm_t(w_ref[hi:, lo:hi], ikk)
            l_ref[hi:, lo:hi] = panel
            w_ref[hi:, hi:] = w_ref[hi:, hi:] - _mm_t(panel, panel)
    for i in range(nb):
        for j in range(i - 1, -1, -1):
            acc = _mm(l_ref[i * BLK:(i + 1) * BLK, j * BLK:i * BLK], inv_ref[j * BLK:i * BLK, j * BLK:(j + 1) * BLK])
            inv_ref[i * BLK:(i + 1) * BLK, j * BLK:(j + 1) * BLK] = -_mm(inv_diag[i], acc)


def factor_and_inverse(sym):
    n = sym.shape[0]
    return pl.pallas_call(
        _factor_kernel,
        out_shape=(jax.ShapeDtypeStruct((n, n), jnp.float32), jax.ShapeDtypeStruct((n, n), jnp.float32)),
        in_specs=[pl.BlockSpec(memory_space=pltpu.VMEM)],
        out_specs=(pl.BlockSpec(memory_space=pltpu.VMEM), pl.BlockSpec(memory_space=pltpu.VMEM)),
        scratch_shapes=[pltpu.VMEM((n, n), jnp.float32)] + [pltpu.VMEM((BLK, BLK), jnp.float32)] * 3,
    )(sym)


def local(front_block, child_blocks, child_rows, child_dest, panel_owner):
    local_rows = front_block[0]
    front_count = lax.axis_size("front")
    blocks = child_blocks[0, 0]
    row_lists = child_rows[0, 0]
    target_front = child_dest[0, 0, :, 0]
    block_count = target_front.shape[0]
    position = jnp.arange(block_count, dtype=jnp.int32)
    same_front = target_front[:, None] == target_front[None, :]
    earlier = position[None, :] < position[:, None]
    slot_index = target_front * CAP + jnp.sum((same_front & earlier).astype(jnp.int32), axis=1)
    send_rows = pack_slots(row_lists, slot_index, front_count)
    send_panel = pack_slots(blocks[:, :, :PB], slot_index, front_count)
    got_panel = lax.all_to_all(send_panel, "front", split_axis=0, concat_axis=0, tiled=True)
    got_rows = lax.all_to_all(send_rows, "front", split_axis=0, concat_axis=0, tiled=True)
    flat_rows = got_rows.reshape(-1)
    panel_part = local_rows[:, :PB].at[flat_rows].add(got_panel.reshape(-1, PB))
    send_trail = pack_slots(blocks[:, :, PB:], slot_index, front_count)
    trailing_rows = lax.all_to_all(send_trail, "front", split_axis=0, concat_axis=0, tiled=True)
    win_cols = local_rows.shape[1] - PB
    owner_index = panel_owner[0]
    is_owner = lax.axis_index("grp") == owner_index

    pivot_block = broadcast_from(panel_part[:PB], owner_index, "grp")
    window_rows = broadcast_from(panel_part[PB:PB + win_cols], owner_index, "grp")
    symmetric = 0.5 * (pivot_block + pivot_block.T)
    pivot_factor, factor_inverse = factor_and_inverse(symmetric)
    solved = jnp.dot(panel_part, factor_inverse.T, precision=FAST)
    window = jnp.dot(window_rows, factor_inverse.T, precision=FAST)
    schur_part = local_rows[:, PB:] - jnp.dot(solved, window.T, precision=FAST)
    schur_part = schur_part.at[flat_rows].add(trailing_rows.reshape(-1, win_cols))
    head = jnp.where(is_owner, pivot_factor, solved[:PB])
    panel_rows = lax.dynamic_update_slice(solved, head, (0, 0))
    return (panel_rows[None], schur_part[None])


def solution(mesh):
    placed = (
        P("front", "grp", None),
        P("front", "grp", None, None, None),
        P("front", "grp", None, None),
        P("front", "grp", None, None),
        P("front"),
    )
    return jax.shard_map(
        local,
        mesh=mesh,
        in_specs=placed,
        out_specs=(P("front", "grp", None), P("front", "grp", None)),
        check_vma=False,
    )
```

```python
import jax
import jax.numpy as jnp
from jax import lax
from jax.experimental import pallas as pl
from jax.experimental.pallas import tpu as pltpu
from jax.sharding import PartitionSpec as P

PB = 512
CAP = 2
BLK = 128
EXACT = lax.Precision.HIGHEST
FAST = lax.Precision.HIGH


def pack_slots(values, slot_index, front_count):
    empty = jnp.zeros((front_count * CAP,) + values.shape[1:], values.dtype)
    filled = empty.at[slot_index].set(values)
    return filled.reshape((front_count, CAP) + values.shape[1:])


def pairs(size, bit):
    return [(d, d ^ bit) for d in range(size)]


def broadcast_from(x, owner, axis):
    size = lax.axis_size(axis)
    me = lax.axis_index(axis)
    got = lax.ppermute(x, axis, pairs(size, 1))
    x = jnp.where(me == owner, x, got)
    half_rows = x.shape[0] // 2
    core = me % 2
    half = jnp.where(core == 0, x[:half_rows], x[half_rows:])
    bit = 2
    while bit < size:
        got = lax.ppermute(half, axis, pairs(size, bit))
        half = jnp.where(me // bit == owner // bit, half, got)
        bit *= 2
    other = lax.ppermute(half, axis, pairs(size, 1))
    return jnp.where(
        core == 0,
        jnp.concatenate([half, other], axis=0),
        jnp.concatenate([other, half], axis=0),
    )


def _mm(a, b):
    return jnp.dot(a, b, precision=EXACT, preferred_element_type=jnp.float32)


def _mm_t(a, b):
    return lax.dot_general(a, b, (((1,), (1,)), ((), ())), precision=EXACT, preferred_element_type=jnp.float32)


def _factor_kernel(s_ref, l_ref, inv_ref, w_ref, d_ref, dt_ref, di_ref):
    n = s_ref.shape[0]
    nb = n // BLK
    w_ref[...] = s_ref[...]
    l_ref[...] = jnp.zeros_like(l_ref)
    inv_ref[...] = jnp.zeros_like(inv_ref)
    sub = lax.broadcasted_iota(jnp.int32, (BLK, BLK), 0)
    lane = lax.broadcasted_iota(jnp.int32, (BLK, BLK), 1)
    lane1 = lax.broadcasted_iota(jnp.int32, (1, BLK), 1)
    sub1 = lax.broadcasted_iota(jnp.int32, (BLK, 1), 0)
    eye = jnp.where(sub == lane, 1.0, 0.0).astype(jnp.float32)

    def step(j, carry):
        row = d_ref[pl.ds(j, 1), :]
        d = jnp.sum(jnp.where(lane1 == j, row, 0.0), axis=1, keepdims=True)
        s = lax.rsqrt(d)
        c = jnp.where(lane1 >= j, row * s, 0.0)
        wv = d_ref[...]
        col = jnp.sum(jnp.where(lane == j, wv, 0.0), axis=1, keepdims=True)
        ccol = jnp.where(sub1 >= j, col * s, 0.0)
        d_ref[...] = wv - ccol * c
        dt_ref[pl.ds(j, 1), :] = c
        xrow = di_ref[pl.ds(j, 1), :] * s
        di_ref[...] = di_ref[...] - jnp.where(sub1 > j, ccol, 0.0) * xrow
        di_ref[pl.ds(j, 1), :] = xrow
        return carry

    inv_diag = []
    for k in range(nb):
        lo, hi = k * BLK, (k + 1) * BLK
        d_ref[...] = w_ref[lo:hi, lo:hi]
        di_ref[...] = eye
        lax.fori_loop(0, BLK, step, 0)
        lkk = dt_ref[...].T
        ikk = di_ref[...]
        l_ref[lo:hi, lo:hi] = lkk
        inv_ref[lo:hi, lo:hi] = ikk
        inv_diag.append(ikk)
        if k + 1 < nb:
            panel = _mm_t(w_ref[hi:, lo:hi], ikk)
            l_ref[hi:, lo:hi] = panel
            w_ref[hi:, hi:] = w_ref[hi:, hi:] - _mm_t(panel, panel)
    for i in range(nb):
        for j in range(i - 1, -1, -1):
            acc = _mm(l_ref[i * BLK:(i + 1) * BLK, j * BLK:i * BLK], inv_ref[j * BLK:i * BLK, j * BLK:(j + 1) * BLK])
            inv_ref[i * BLK:(i + 1) * BLK, j * BLK:(j + 1) * BLK] = -_mm(inv_diag[i], acc)


def factor_and_inverse(sym):
    n = sym.shape[0]
    return pl.pallas_call(
        _factor_kernel,
        out_shape=(jax.ShapeDtypeStruct((n, n), jnp.float32), jax.ShapeDtypeStruct((n, n), jnp.float32)),
        in_specs=[pl.BlockSpec(memory_space=pltpu.VMEM)],
        out_specs=(pl.BlockSpec(memory_space=pltpu.VMEM), pl.BlockSpec(memory_space=pltpu.VMEM)),
        scratch_shapes=[pltpu.VMEM((n, n), jnp.float32)] + [pltpu.VMEM((BLK, BLK), jnp.float32)] * 3,
    )(sym)


def local(front_block, child_blocks, child_rows, child_dest, panel_owner):
    local_rows = front_block[0]
    front_count = lax.axis_size("front")
    blocks = child_blocks[0, 0]
    row_lists = child_rows[0, 0]
    target_front = child_dest[0, 0, :, 0]
    block_count = target_front.shape[0]
    position = jnp.arange(block_count, dtype=jnp.int32)
    same_front = target_front[:, None] == target_front[None, :]
    earlier = position[None, :] < position[:, None]
    slot_index = target_front * CAP + jnp.sum((same_front & earlier).astype(jnp.int32), axis=1)
    send_rows = pack_slots(row_lists, slot_index, front_count)
    send_panel = pack_slots(blocks[:, :, :PB], slot_index, front_count)
    got_panel = lax.all_to_all(send_panel, "front", split_axis=0, concat_axis=0, tiled=True)
    got_rows = lax.all_to_all(send_rows, "front", split_axis=0, concat_axis=0, tiled=True)
    flat_rows = got_rows.reshape(-1)
    panel_part = local_rows[:, :PB].at[flat_rows].add(got_panel.reshape(-1, PB))
    send_trail = pack_slots(blocks[:, :, PB:], slot_index, front_count)
    trailing_rows = lax.all_to_all(send_trail, "front", split_axis=0, concat_axis=0, tiled=True)
    win_cols = local_rows.shape[1] - PB
    owner_index = panel_owner[0]
    is_owner = lax.axis_index("grp") == owner_index

    top_count = PB + win_cols
    top_hits = (jnp.arange(top_count, dtype=jnp.int32)[:, None] == flat_rows[None, :]).astype(jnp.float32)
    top_front = lax.optimization_barrier(front_block[0, :top_count, :PB])
    top_rows = top_front + jnp.dot(top_hits, got_panel.reshape(-1, PB), precision=EXACT)
    pivot_block = broadcast_from(top_rows[:PB], owner_index, "grp")
    window_rows = broadcast_from(top_rows[PB:], owner_index, "grp")
    symmetric = 0.5 * (pivot_block + pivot_block.T)
    pivot_factor, factor_inverse = factor_and_inverse(symmetric)
    solved = jnp.dot(panel_part, factor_inverse.T, precision=FAST)
    window = jnp.dot(window_rows, factor_inverse.T, precision=FAST)
    schur_part = local_rows[:, PB:] - jnp.dot(solved, window.T, precision=FAST)
    schur_part = schur_part.at[flat_rows].add(trailing_rows.reshape(-1, win_cols))
    head = jnp.where(is_owner, pivot_factor, solved[:PB])
    panel_rows = lax.dynamic_update_slice(solved, head, (0, 0))
    return (panel_rows[None], schur_part[None])


def solution(mesh):
    placed = (
        P("front", "grp", None),
        P("front", "grp", None, None, None),
        P("front", "grp", None, None),
        P("front", "grp", None, None),
        P("front"),
    )
    return jax.shard_map(
        local,
        mesh=mesh,
        in_specs=placed,
        out_specs=(P("front", "grp", None), P("front", "grp", None)),
        check_vma=False,
    )
```

```python
import jax
import jax.numpy as jnp
from jax import lax
from jax.experimental import pallas as pl
from jax.experimental.pallas import tpu as pltpu
from jax.sharding import PartitionSpec as P

PB = 512
CAP = 2
BLK = 128
EXACT = lax.Precision.HIGHEST
FAST = lax.Precision.HIGH


def pack_slots(values, slot_index, front_count):
    empty = jnp.zeros((front_count * CAP,) + values.shape[1:], values.dtype)
    filled = empty.at[slot_index].set(values)
    return filled.reshape((front_count, CAP) + values.shape[1:])


def pairs(size, bit):
    return [(d, d ^ bit) for d in range(size)]


def broadcast_from(x, owner, axis):
    size = lax.axis_size(axis)
    me = lax.axis_index(axis)
    got = lax.ppermute(x, axis, pairs(size, 1))
    x = jnp.where(me == owner, x, got)
    half_rows = x.shape[0] // 2
    core = me % 2
    half = jnp.where(core == 0, x[:half_rows], x[half_rows:])
    bit = 2
    while bit < size:
        got = lax.ppermute(half, axis, pairs(size, bit))
        half = jnp.where(me // bit == owner // bit, half, got)
        bit *= 2
    other = lax.ppermute(half, axis, pairs(size, 1))
    return jnp.where(
        core == 0,
        jnp.concatenate([half, other], axis=0),
        jnp.concatenate([other, half], axis=0),
    )


def _mm(a, b):
    return jnp.dot(a, b, precision=EXACT, preferred_element_type=jnp.float32)


def _mm_t(a, b):
    return lax.dot_general(a, b, (((1,), (1,)), ((), ())), precision=EXACT, preferred_element_type=jnp.float32)


def _factor_kernel(s_ref, l_ref, inv_ref, w_ref, d_ref, dt_ref, di_ref):
    n = s_ref.shape[0]
    nb = n // BLK
    w_ref[...] = s_ref[...]
    l_ref[...] = jnp.zeros_like(l_ref)
    inv_ref[...] = jnp.zeros_like(inv_ref)
    sub = lax.broadcasted_iota(jnp.int32, (BLK, BLK), 0)
    lane = lax.broadcasted_iota(jnp.int32, (BLK, BLK), 1)
    lane1 = lax.broadcasted_iota(jnp.int32, (1, BLK), 1)
    sub1 = lax.broadcasted_iota(jnp.int32, (BLK, 1), 0)
    eye = jnp.where(sub == lane, 1.0, 0.0).astype(jnp.float32)

    def step(t, carry):
        j = 2 * t
        r0 = d_ref[pl.ds(j, 1), :]
        r1 = d_ref[pl.ds(j + 1, 1), :]
        d0 = jnp.sum(jnp.where(lane1 == j, r0, 0.0), axis=1, keepdims=True)
        e = jnp.sum(jnp.where(lane1 == j, r1, 0.0), axis=1, keepdims=True)
        d1 = jnp.sum(jnp.where(lane1 == j + 1, r1, 0.0), axis=1, keepdims=True)
        s0 = lax.rsqrt(d0)
        l10 = e * s0
        s1 = lax.rsqrt(d1 - l10 * l10)
        c0 = jnp.where(lane1 >= j, r0 * s0, 0.0)
        c1 = jnp.where(lane1 >= j + 1, (r1 - l10 * c0) * s1, 0.0)
        wv = d_ref[...]
        col0 = jnp.sum(jnp.where(lane == j, wv, 0.0), axis=1, keepdims=True)
        col1 = jnp.sum(jnp.where(lane == j + 1, wv, 0.0), axis=1, keepdims=True)
        ccol0 = jnp.where(sub1 >= j, col0 * s0, 0.0)
        ccol1 = jnp.where(sub1 >= j + 1, (col1 - l10 * ccol0) * s1, 0.0)
        d_ref[...] = wv - ccol0 * c0 - ccol1 * c1
        dt_ref[pl.ds(j, 1), :] = c0
        dt_ref[pl.ds(j + 1, 1), :] = c1
        x0 = di_ref[pl.ds(j, 1), :] * s0
        x1 = (di_ref[pl.ds(j + 1, 1), :] - l10 * x0) * s1
        below = sub1 > j + 1
        di_ref[...] = di_ref[...] - jnp.where(below, ccol0, 0.0) * x0 - jnp.where(below, ccol1, 0.0) * x1
        di_ref[pl.ds(j, 1), :] = x0
        di_ref[pl.ds(j + 1, 1), :] = x1
        return carry

    inv_diag = []
    for k in range(nb):
        lo, hi = k * BLK, (k + 1) * BLK
        d_ref[...] = w_ref[lo:hi, lo:hi]
        di_ref[...] = eye
        lax.fori_loop(0, BLK // 2, step, 0)
        lkk = dt_ref[...].T
        ikk = di_ref[...]
        l_ref[lo:hi, lo:hi] = lkk
        inv_ref[lo:hi, lo:hi] = ikk
        inv_diag.append(ikk)
        if k + 1 < nb:
            panel = _mm_t(w_ref[hi:, lo:hi], ikk)
            l_ref[hi:, lo:hi] = panel
            w_ref[hi:, hi:] = w_ref[hi:, hi:] - _mm_t(panel, panel)
    for i in range(nb):
        for j in range(i - 1, -1, -1):
            acc = _mm(l_ref[i * BLK:(i + 1) * BLK, j * BLK:i * BLK], inv_ref[j * BLK:i * BLK, j * BLK:(j + 1) * BLK])
            inv_ref[i * BLK:(i + 1) * BLK, j * BLK:(j + 1) * BLK] = -_mm(inv_diag[i], acc)


def factor_and_inverse(sym):
    n = sym.shape[0]
    return pl.pallas_call(
        _factor_kernel,
        out_shape=(jax.ShapeDtypeStruct((n, n), jnp.float32), jax.ShapeDtypeStruct((n, n), jnp.float32)),
        in_specs=[pl.BlockSpec(memory_space=pltpu.VMEM)],
        out_specs=(pl.BlockSpec(memory_space=pltpu.VMEM), pl.BlockSpec(memory_space=pltpu.VMEM)),
        scratch_shapes=[pltpu.VMEM((n, n), jnp.float32)] + [pltpu.VMEM((BLK, BLK), jnp.float32)] * 3,
    )(sym)


def local(front_block, child_blocks, child_rows, child_dest, panel_owner):
    local_rows = front_block[0]
    front_count = lax.axis_size("front")
    blocks = child_blocks[0, 0]
    row_lists = child_rows[0, 0]
    target_front = child_dest[0, 0, :, 0]
    block_count = target_front.shape[0]
    position = jnp.arange(block_count, dtype=jnp.int32)
    same_front = target_front[:, None] == target_front[None, :]
    earlier = position[None, :] < position[:, None]
    slot_index = target_front * CAP + jnp.sum((same_front & earlier).astype(jnp.int32), axis=1)
    send_rows = pack_slots(row_lists, slot_index, front_count)
    send_panel = pack_slots(blocks[:, :, :PB], slot_index, front_count)
    got_panel = lax.all_to_all(send_panel, "front", split_axis=0, concat_axis=0, tiled=True)
    got_rows = lax.all_to_all(send_rows, "front", split_axis=0, concat_axis=0, tiled=True)
    flat_rows = got_rows.reshape(-1)
    panel_part = local_rows[:, :PB].at[flat_rows].add(got_panel.reshape(-1, PB))
    send_trail = pack_slots(blocks[:, :, PB:], slot_index, front_count)
    trailing_rows = lax.all_to_all(send_trail, "front", split_axis=0, concat_axis=0, tiled=True)
    win_cols = local_rows.shape[1] - PB
    owner_index = panel_owner[0]
    is_owner = lax.axis_index("grp") == owner_index

    pivot_block = broadcast_from(panel_part[:PB], owner_index, "grp")
    window_rows = broadcast_from(panel_part[PB:PB + win_cols], owner_index, "grp")
    symmetric = 0.5 * (pivot_block + pivot_block.T)
    pivot_factor, factor_inverse = factor_and_inverse(symmetric)
    solved = jnp.dot(panel_part, factor_inverse.T, precision=FAST)
    window = jnp.dot(window_rows, factor_inverse.T, precision=FAST)
    schur_part = local_rows[:, PB:] - jnp.dot(solved, window.T, precision=FAST)
    schur_part = schur_part.at[flat_rows].add(trailing_rows.reshape(-1, win_cols))
    head = jnp.where(is_owner, pivot_factor, solved[:PB])
    panel_rows = lax.dynamic_update_slice(solved, head, (0, 0))
    return (panel_rows[None], schur_part[None])


def solution(mesh):
    placed = (
        P("front", "grp", None),
        P("front", "grp", None, None, None),
        P("front", "grp", None, None),
        P("front", "grp", None, None),
        P("front"),
    )
    return jax.shard_map(
        local,
        mesh=mesh,
        in_specs=placed,
        out_specs=(P("front", "grp", None), P("front", "grp", None)),
        check_vma=False,
    )
```

```python
import jax
import jax.numpy as jnp
from jax import lax
from jax.experimental import pallas as pl
from jax.experimental.pallas import tpu as pltpu
from jax.sharding import PartitionSpec as P

PB = 512
CAP = 2
BLK = 128
EXACT = lax.Precision.HIGHEST
FAST = lax.Precision.HIGH


def pack_slots(values, slot_index, front_count):
    empty = jnp.zeros((front_count * CAP,) + values.shape[1:], values.dtype)
    filled = empty.at[slot_index].set(values)
    return filled.reshape((front_count, CAP) + values.shape[1:])


def pairs(size, bit):
    return [(d, d ^ bit) for d in range(size)]


def broadcast_from(x, owner, axis):
    size = lax.axis_size(axis)
    me = lax.axis_index(axis)
    got = lax.ppermute(x, axis, pairs(size, 1))
    x = jnp.where(me == owner, x, got)
    half_rows = x.shape[0] // 2
    core = me % 2
    half = jnp.where(core == 0, x[:half_rows], x[half_rows:])
    bit = 2
    while bit < size:
        got = lax.ppermute(half, axis, pairs(size, bit))
        half = jnp.where(me // bit == owner // bit, half, got)
        bit *= 2
    other = lax.ppermute(half, axis, pairs(size, 1))
    return jnp.where(
        core == 0,
        jnp.concatenate([half, other], axis=0),
        jnp.concatenate([other, half], axis=0),
    )


def _mm(a, b):
    return jnp.dot(a, b, precision=EXACT, preferred_element_type=jnp.float32)


def _mm_t(a, b):
    return lax.dot_general(a, b, (((1,), (1,)), ((), ())), precision=EXACT, preferred_element_type=jnp.float32)


def _factor_kernel(s_ref, l_ref, inv_ref, w_ref, d_ref, dt_ref, di_ref):
    n = s_ref.shape[0]
    nb = n // BLK
    w_ref[...] = s_ref[...]
    l_ref[...] = jnp.zeros_like(l_ref)
    inv_ref[...] = jnp.zeros_like(inv_ref)
    sub = lax.broadcasted_iota(jnp.int32, (BLK, BLK), 0)
    lane = lax.broadcasted_iota(jnp.int32, (BLK, BLK), 1)
    lane1 = lax.broadcasted_iota(jnp.int32, (1, BLK), 1)
    sub1 = lax.broadcasted_iota(jnp.int32, (BLK, 1), 0)
    eye = jnp.where(sub == lane, 1.0, 0.0).astype(jnp.float32)

    def step(t, carry):
        j = 2 * t
        r0 = d_ref[pl.ds(j, 1), :]
        r1 = d_ref[pl.ds(j + 1, 1), :]
        d0 = jnp.sum(jnp.where(lane1 == j, r0, 0.0), axis=1, keepdims=True)
        e = jnp.sum(jnp.where(lane1 == j, r1, 0.0), axis=1, keepdims=True)
        d1 = jnp.sum(jnp.where(lane1 == j + 1, r1, 0.0), axis=1, keepdims=True)
        s0 = lax.rsqrt(d0)
        l10 = e * s0
        s1 = lax.rsqrt(d1 - l10 * l10)
        c0 = jnp.where(lane1 >= j, r0 * s0, 0.0)
        c1 = jnp.where(lane1 >= j + 1, (r1 - l10 * c0) * s1, 0.0)
        wv = d_ref[...]
        col0 = jnp.sum(jnp.where(lane == j, wv, 0.0), axis=1, keepdims=True)
        col1 = jnp.sum(jnp.where(lane == j + 1, wv, 0.0), axis=1, keepdims=True)
        ccol0 = jnp.where(sub1 >= j, col0 * s0, 0.0)
        ccol1 = jnp.where(sub1 >= j + 1, (col1 - l10 * ccol0) * s1, 0.0)
        d_ref[...] = wv - ccol0 * c0 - ccol1 * c1
        dt_ref[pl.ds(j, 1), :] = c0
        dt_ref[pl.ds(j + 1, 1), :] = c1
        x0 = di_ref[pl.ds(j, 1), :] * s0
        x1 = (di_ref[pl.ds(j + 1, 1), :] - l10 * x0) * s1
        below = sub1 > j + 1
        di_ref[...] = di_ref[...] - jnp.where(below, ccol0, 0.0) * x0 - jnp.where(below, ccol1, 0.0) * x1
        di_ref[pl.ds(j, 1), :] = x0
        di_ref[pl.ds(j + 1, 1), :] = x1
        return carry

    inv_diag = []
    for k in range(nb):
        lo, hi = k * BLK, (k + 1) * BLK
        d_ref[...] = w_ref[lo:hi, lo:hi]
        di_ref[...] = eye
        lax.fori_loop(0, BLK // 2, step, 0)
        lkk = dt_ref[...].T
        ikk = di_ref[...]
        l_ref[lo:hi, lo:hi] = lkk
        inv_ref[lo:hi, lo:hi] = ikk
        inv_diag.append(ikk)
        if k + 1 < nb:
            panel = _mm_t(w_ref[hi:, lo:hi], ikk)
            l_ref[hi:, lo:hi] = panel
            w_ref[hi:, hi:] = w_ref[hi:, hi:] - _mm_t(panel, panel)
    for i in range(nb):
        for j in range(i - 1, -1, -1):
            acc = _mm(l_ref[i * BLK:(i + 1) * BLK, j * BLK:i * BLK], inv_ref[j * BLK:i * BLK, j * BLK:(j + 1) * BLK])
            inv_ref[i * BLK:(i + 1) * BLK, j * BLK:(j + 1) * BLK] = -_mm(inv_diag[i], acc)


def factor_and_inverse(sym):
    n = sym.shape[0]
    return pl.pallas_call(
        _factor_kernel,
        out_shape=(jax.ShapeDtypeStruct((n, n), jnp.float32), jax.ShapeDtypeStruct((n, n), jnp.float32)),
        in_specs=[pl.BlockSpec(memory_space=pltpu.VMEM)],
        out_specs=(pl.BlockSpec(memory_space=pltpu.VMEM), pl.BlockSpec(memory_space=pltpu.VMEM)),
        scratch_shapes=[pltpu.VMEM((n, n), jnp.float32)] + [pltpu.VMEM((BLK, BLK), jnp.float32)] * 3,
    )(sym)


def _row_add_kernel(idx_ref, lead_ref, base_ref, add_ref, out_ref, buf, sems):
    count = add_ref.shape[0]

    def fetch(i):
        return pltpu.make_async_copy(base_ref.at[pl.ds(idx_ref[i], 1)], buf.at[pl.ds(i, 1)], sems.at[i])

    def store(i):
        return pltpu.make_async_copy(buf.at[pl.ds(i, 1)], out_ref.at[pl.ds(idx_ref[i], 1)], sems.at[i])

    def start_fetch(i, c):
        fetch(i).start()
        return c

    def wait_fetch(i, c):
        fetch(i).wait()
        return c

    lax.fori_loop(0, count, start_fetch, 0)
    lax.fori_loop(0, count, wait_fetch, 0)

    def accumulate(i, c):
        lead = lead_ref[i]
        buf[pl.ds(lead, 1), :] = buf[pl.ds(lead, 1), :] + add_ref[pl.ds(i, 1), :]
        return c

    lax.fori_loop(0, count, accumulate, 0)

    def start_store(i, c):
        @pl.when(lead_ref[i] == i)
        def _():
            store(i).start()
        return c

    def wait_store(i, c):
        @pl.when(lead_ref[i] == i)
        def _():
            store(i).wait()
        return c

    lax.fori_loop(0, count, start_store, 0)
    lax.fori_loop(0, count, wait_store, 0)


def add_rows(base, rows, values):
    count, width = values.shape
    same = rows[:, None] == rows[None, :]
    lead = jnp.argmax(same, axis=1).astype(jnp.int32)
    return pl.pallas_call(
        _row_add_kernel,
        out_shape=jax.ShapeDtypeStruct(base.shape, base.dtype),
        in_specs=[
            pl.BlockSpec(memory_space=pltpu.SMEM),
            pl.BlockSpec(memory_space=pltpu.SMEM),
            pl.BlockSpec(memory_space=pl.ANY),
            pl.BlockSpec(memory_space=pltpu.VMEM),
        ],
        out_specs=pl.BlockSpec(memory_space=pl.ANY),
        scratch_shapes=[pltpu.VMEM((count, width), jnp.float32), pltpu.SemaphoreType.DMA((count,))],
        input_output_aliases={2: 0},
    )(rows, lead, base, values)


def local(front_block, child_blocks, child_rows, child_dest, panel_owner):
    local_rows = front_block[0]
    front_count = lax.axis_size("front")
    blocks = child_blocks[0, 0]
    row_lists = child_rows[0, 0]
    target_front = child_dest[0, 0, :, 0]
    block_count = target_front.shape[0]
    position = jnp.arange(block_count, dtype=jnp.int32)
    same_front = target_front[:, None] == target_front[None, :]
    earlier = position[None, :] < position[:, None]
    slot_index = target_front * CAP + jnp.sum((same_front & earlier).astype(jnp.int32), axis=1)
    send_rows = pack_slots(row_lists, slot_index, front_count)
    send_panel = pack_slots(blocks[:, :, :PB], slot_index, front_count)
    got_panel = lax.all_to_all(send_panel, "front", split_axis=0, concat_axis=0, tiled=True)
    got_rows = lax.all_to_all(send_rows, "front", split_axis=0, concat_axis=0, tiled=True)
    flat_rows = got_rows.reshape(-1)
    panel_part = add_rows(local_rows[:, :PB], flat_rows, got_panel.reshape(-1, PB))
    send_trail = pack_slots(blocks[:, :, PB:], slot_index, front_count)
    trailing_rows = lax.all_to_all(send_trail, "front", split_axis=0, concat_axis=0, tiled=True)
    win_cols = local_rows.shape[1] - PB
    owner_index = panel_owner[0]
    is_owner = lax.axis_index("grp") == owner_index

    pivot_block = broadcast_from(panel_part[:PB], owner_index, "grp")
    window_rows = broadcast_from(panel_part[PB:PB + win_cols], owner_index, "grp")
    symmetric = 0.5 * (pivot_block + pivot_block.T)
    pivot_factor, factor_inverse = factor_and_inverse(symmetric)
    solved = jnp.dot(panel_part, factor_inverse.T, precision=FAST)
    window = jnp.dot(window_rows, factor_inverse.T, precision=FAST)
    schur_part = local_rows[:, PB:] - jnp.dot(solved, window.T, precision=FAST)
    schur_part = add_rows(schur_part, flat_rows, trailing_rows.reshape(-1, win_cols))
    head = jnp.where(is_owner, pivot_factor, solved[:PB])
    panel_rows = lax.dynamic_update_slice(solved, head, (0, 0))
    return (panel_rows[None], schur_part[None])


def solution(mesh):
    placed = (
        P("front", "grp", None),
        P("front", "grp", None, None, None),
        P("front", "grp", None, None),
        P("front", "grp", None, None),
        P("front"),
    )
    return jax.shard_map(
        local,
        mesh=mesh,
        in_specs=placed,
        out_specs=(P("front", "grp", None), P("front", "grp", None)),
        check_vma=False,
    )
```

```python
import functools

import jax
import jax.numpy as jnp
from jax import lax
from jax.experimental import pallas as pl
from jax.experimental.pallas import tpu as pltpu
from jax.sharding import PartitionSpec as P

PB = 512
CAP = 2
BLK = 128
EXACT = lax.Precision.HIGHEST
FAST = lax.Precision.HIGH


def pack_slots(values, slot_index, front_count):
    empty = jnp.zeros((front_count * CAP,) + values.shape[1:], values.dtype)
    filled = empty.at[slot_index].set(values)
    return filled.reshape((front_count, CAP) + values.shape[1:])


def pairs(size, bit):
    return [(d, d ^ bit) for d in range(size)]


def broadcast_from(x, owner, axis):
    size = lax.axis_size(axis)
    me = lax.axis_index(axis)
    got = lax.ppermute(x, axis, pairs(size, 1))
    x = jnp.where(me == owner, x, got)
    half_rows = x.shape[0] // 2
    core = me % 2
    half = jnp.where(core == 0, x[:half_rows], x[half_rows:])
    bit = 2
    while bit < size:
        got = lax.ppermute(half, axis, pairs(size, bit))
        half = jnp.where(me // bit == owner // bit, half, got)
        bit *= 2
    other = lax.ppermute(half, axis, pairs(size, 1))
    return jnp.where(
        core == 0,
        jnp.concatenate([half, other], axis=0),
        jnp.concatenate([other, half], axis=0),
    )


def _mm(a, b):
    return jnp.dot(a, b, precision=EXACT, preferred_element_type=jnp.float32)


def _mm_t(a, b):
    return lax.dot_general(a, b, (((1,), (1,)), ((), ())), precision=EXACT, preferred_element_type=jnp.float32)


def _factor_kernel(s_ref, l_ref, inv_ref, w_ref, d_ref, dt_ref, di_ref):
    n = s_ref.shape[0]
    nb = n // BLK
    w_ref[...] = s_ref[...]
    l_ref[...] = jnp.zeros_like(l_ref)
    inv_ref[...] = jnp.zeros_like(inv_ref)
    sub = lax.broadcasted_iota(jnp.int32, (BLK, BLK), 0)
    lane = lax.broadcasted_iota(jnp.int32, (BLK, BLK), 1)
    lane1 = lax.broadcasted_iota(jnp.int32, (1, BLK), 1)
    sub1 = lax.broadcasted_iota(jnp.int32, (BLK, 1), 0)
    eye = jnp.where(sub == lane, 1.0, 0.0).astype(jnp.float32)

    def step(t, carry):
        j = 2 * t
        r0 = d_ref[pl.ds(j, 1), :]
        r1 = d_ref[pl.ds(j + 1, 1), :]
        d0 = jnp.sum(jnp.where(lane1 == j, r0, 0.0), axis=1, keepdims=True)
        e = jnp.sum(jnp.where(lane1 == j, r1, 0.0), axis=1, keepdims=True)
        d1 = jnp.sum(jnp.where(lane1 == j + 1, r1, 0.0), axis=1, keepdims=True)
        s0 = lax.rsqrt(d0)
        l10 = e * s0
        s1 = lax.rsqrt(d1 - l10 * l10)
        c0 = jnp.where(lane1 >= j, r0 * s0, 0.0)
        c1 = jnp.where(lane1 >= j + 1, (r1 - l10 * c0) * s1, 0.0)
        wv = d_ref[...]
        col0 = jnp.sum(jnp.where(lane == j, wv, 0.0), axis=1, keepdims=True)
        col1 = jnp.sum(jnp.where(lane == j + 1, wv, 0.0), axis=1, keepdims=True)
        ccol0 = jnp.where(sub1 >= j, col0 * s0, 0.0)
        ccol1 = jnp.where(sub1 >= j + 1, (col1 - l10 * ccol0) * s1, 0.0)
        d_ref[...] = wv - ccol0 * c0 - ccol1 * c1
        dt_ref[pl.ds(j, 1), :] = c0
        dt_ref[pl.ds(j + 1, 1), :] = c1
        x0 = di_ref[pl.ds(j, 1), :] * s0
        x1 = (di_ref[pl.ds(j + 1, 1), :] - l10 * x0) * s1
        below = sub1 > j + 1
        di_ref[...] = di_ref[...] - jnp.where(below, ccol0, 0.0) * x0 - jnp.where(below, ccol1, 0.0) * x1
        di_ref[pl.ds(j, 1), :] = x0
        di_ref[pl.ds(j + 1, 1), :] = x1
        return carry

    inv_diag = []
    for k in range(nb):
        lo, hi = k * BLK, (k + 1) * BLK
        d_ref[...] = w_ref[lo:hi, lo:hi]
        di_ref[...] = eye
        lax.fori_loop(0, BLK // 2, step, 0)
        lkk = dt_ref[...].T
        ikk = di_ref[...]
        l_ref[lo:hi, lo:hi] = lkk
        inv_ref[lo:hi, lo:hi] = ikk
        inv_diag.append(ikk)
        if k + 1 < nb:
            panel = _mm_t(w_ref[hi:, lo:hi], ikk)
            l_ref[hi:, lo:hi] = panel
            w_ref[hi:, hi:] = w_ref[hi:, hi:] - _mm_t(panel, panel)
    for i in range(nb):
        for j in range(i - 1, -1, -1):
            acc = _mm(l_ref[i * BLK:(i + 1) * BLK, j * BLK:i * BLK], inv_ref[j * BLK:i * BLK, j * BLK:(j + 1) * BLK])
            inv_ref[i * BLK:(i + 1) * BLK, j * BLK:(j + 1) * BLK] = -_mm(inv_diag[i], acc)


def factor_and_inverse(sym):
    n = sym.shape[0]
    return pl.pallas_call(
        _factor_kernel,
        out_shape=(jax.ShapeDtypeStruct((n, n), jnp.float32), jax.ShapeDtypeStruct((n, n), jnp.float32)),
        in_specs=[pl.BlockSpec(memory_space=pltpu.VMEM)],
        out_specs=(pl.BlockSpec(memory_space=pltpu.VMEM), pl.BlockSpec(memory_space=pltpu.VMEM)),
        scratch_shapes=[pltpu.VMEM((n, n), jnp.float32)] + [pltpu.VMEM((BLK, BLK), jnp.float32)] * 3,
    )(sym)


def _block_add_kernel(col0, idx_ref, base_ref, add_ref, out_ref, sem):
    width = out_ref.shape[1]
    copy = pltpu.make_async_copy(base_ref.at[:, pl.ds(col0, width)], out_ref, sem)
    copy.start()
    copy.wait()

    def accumulate(i, c):
        r = idx_ref[i]
        out_ref[pl.ds(r, 1), :] = out_ref[pl.ds(r, 1), :] + add_ref[pl.ds(i, 1), :]
        return c

    lax.fori_loop(0, add_ref.shape[0], accumulate, 0)


def add_rows(base, col0, width, rows, values):
    return pl.pallas_call(
        functools.partial(_block_add_kernel, col0),
        out_shape=jax.ShapeDtypeStruct((base.shape[0], width), base.dtype),
        in_specs=[
            pl.BlockSpec(memory_space=pltpu.SMEM),
            pl.BlockSpec(memory_space=pl.ANY),
            pl.BlockSpec(memory_space=pltpu.VMEM),
        ],
        out_specs=pl.BlockSpec(memory_space=pltpu.VMEM),
        scratch_shapes=[pltpu.SemaphoreType.DMA(())],
    )(rows, base, values)


def local(front_block, child_blocks, child_rows, child_dest, panel_owner):
    local_rows = front_block[0]
    front_count = lax.axis_size("front")
    blocks = child_blocks[0, 0]
    row_lists = child_rows[0, 0]
    target_front = child_dest[0, 0, :, 0]
    block_count = target_front.shape[0]
    position = jnp.arange(block_count, dtype=jnp.int32)
    same_front = target_front[:, None] == target_front[None, :]
    earlier = position[None, :] < position[:, None]
    slot_index = target_front * CAP + jnp.sum((same_front & earlier).astype(jnp.int32), axis=1)
    send_rows = pack_slots(row_lists, slot_index, front_count)
    send_panel = pack_slots(blocks[:, :, :PB], slot_index, front_count)
    got_panel = lax.all_to_all(send_panel, "front", split_axis=0, concat_axis=0, tiled=True)
    got_rows = lax.all_to_all(send_rows, "front", split_axis=0, concat_axis=0, tiled=True)
    flat_rows = got_rows.reshape(-1)
    panel_part = add_rows(local_rows, 0, PB, flat_rows, got_panel.reshape(-1, PB))
    send_trail = pack_slots(blocks[:, :, PB:], slot_index, front_count)
    trailing_rows = lax.all_to_all(send_trail, "front", split_axis=0, concat_axis=0, tiled=True)
    win_cols = local_rows.shape[1] - PB
    owner_index = panel_owner[0]
    is_owner = lax.axis_index("grp") == owner_index

    pivot_block = broadcast_from(panel_part[:PB], owner_index, "grp")
    window_rows = broadcast_from(panel_part[PB:PB + win_cols], owner_index, "grp")
    symmetric = 0.5 * (pivot_block + pivot_block.T)
    pivot_factor, factor_inverse = factor_and_inverse(symmetric)
    solved = jnp.dot(panel_part, factor_inverse.T, precision=FAST)
    window = jnp.dot(window_rows, factor_inverse.T, precision=FAST)
    schur_part = local_rows[:, PB:] - jnp.dot(solved, window.T, precision=FAST)
    schur_part = add_rows(schur_part, 0, win_cols, flat_rows, trailing_rows.reshape(-1, win_cols))
    head = jnp.where(is_owner, pivot_factor, solved[:PB])
    panel_rows = lax.dynamic_update_slice(solved, head, (0, 0))
    return (panel_rows[None], schur_part[None])


def solution(mesh):
    placed = (
        P("front", "grp", None),
        P("front", "grp", None, None, None),
        P("front", "grp", None, None),
        P("front", "grp", None, None),
        P("front"),
    )
    return jax.shard_map(
        local,
        mesh=mesh,
        in_specs=placed,
        out_specs=(P("front", "grp", None), P("front", "grp", None)),
        check_vma=False,
    )
```

```python
import functools

import jax
import jax.numpy as jnp
from jax import lax
from jax.experimental import pallas as pl
from jax.experimental.pallas import tpu as pltpu
from jax.sharding import PartitionSpec as P

PB = 512
CAP = 2
BLK = 128
EXACT = lax.Precision.HIGHEST
FAST = lax.Precision.HIGH


def pack_slots(values, slot_index, front_count):
    empty = jnp.zeros((front_count * CAP,) + values.shape[1:], values.dtype)
    filled = empty.at[slot_index].set(values)
    return filled.reshape((front_count, CAP) + values.shape[1:])


def pairs(size, bit):
    return [(d, d ^ bit) for d in range(size)]


def broadcast_from(x, owner, axis):
    size = lax.axis_size(axis)
    me = lax.axis_index(axis)
    got = lax.ppermute(x, axis, pairs(size, 1))
    x = jnp.where(me == owner, x, got)
    half_rows = x.shape[0] // 2
    core = me % 2
    half = jnp.where(core == 0, x[:half_rows], x[half_rows:])
    bit = 2
    while bit < size:
        got = lax.ppermute(half, axis, pairs(size, bit))
        half = jnp.where(me // bit == owner // bit, half, got)
        bit *= 2
    other = lax.ppermute(half, axis, pairs(size, 1))
    return jnp.where(
        core == 0,
        jnp.concatenate([half, other], axis=0),
        jnp.concatenate([other, half], axis=0),
    )


def _mm(a, b):
    return jnp.dot(a, b, precision=EXACT, preferred_element_type=jnp.float32)


def _mm_t(a, b):
    return lax.dot_general(a, b, (((1,), (1,)), ((), ())), precision=EXACT, preferred_element_type=jnp.float32)


def _factor_kernel(s_ref, l_ref, inv_ref, w_ref, d_ref, dt_ref, di_ref):
    n = s_ref.shape[0]
    nb = n // BLK
    w_ref[...] = s_ref[...]
    l_ref[...] = jnp.zeros_like(l_ref)
    inv_ref[...] = jnp.zeros_like(inv_ref)
    sub = lax.broadcasted_iota(jnp.int32, (BLK, BLK), 0)
    lane = lax.broadcasted_iota(jnp.int32, (BLK, BLK), 1)
    lane1 = lax.broadcasted_iota(jnp.int32, (1, BLK), 1)
    sub1 = lax.broadcasted_iota(jnp.int32, (BLK, 1), 0)
    eye = jnp.where(sub == lane, 1.0, 0.0).astype(jnp.float32)

    def step(t, carry):
        j = 2 * t
        r0 = d_ref[pl.ds(j, 1), :]
        r1 = d_ref[pl.ds(j + 1, 1), :]
        d0 = jnp.sum(jnp.where(lane1 == j, r0, 0.0), axis=1, keepdims=True)
        e = jnp.sum(jnp.where(lane1 == j, r1, 0.0), axis=1, keepdims=True)
        d1 = jnp.sum(jnp.where(lane1 == j + 1, r1, 0.0), axis=1, keepdims=True)
        s0 = lax.rsqrt(d0)
        l10 = e * s0
        s1 = lax.rsqrt(d1 - l10 * l10)
        c0 = jnp.where(lane1 >= j, r0 * s0, 0.0)
        c1 = jnp.where(lane1 >= j + 1, (r1 - l10 * c0) * s1, 0.0)
        wv = d_ref[...]
        col0 = jnp.sum(jnp.where(lane == j, wv, 0.0), axis=1, keepdims=True)
        col1 = jnp.sum(jnp.where(lane == j + 1, wv, 0.0), axis=1, keepdims=True)
        ccol0 = jnp.where(sub1 >= j, col0 * s0, 0.0)
        ccol1 = jnp.where(sub1 >= j + 1, (col1 - l10 * ccol0) * s1, 0.0)
        d_ref[...] = wv - ccol0 * c0 - ccol1 * c1
        dt_ref[pl.ds(j, 1), :] = c0
        dt_ref[pl.ds(j + 1, 1), :] = c1
        x0 = di_ref[pl.ds(j, 1), :] * s0
        x1 = (di_ref[pl.ds(j + 1, 1), :] - l10 * x0) * s1
        below = sub1 > j + 1
        di_ref[...] = di_ref[...] - jnp.where(below, ccol0, 0.0) * x0 - jnp.where(below, ccol1, 0.0) * x1
        di_ref[pl.ds(j, 1), :] = x0
        di_ref[pl.ds(j + 1, 1), :] = x1
        return carry

    inv_diag = []
    for k in range(nb):
        lo, hi = k * BLK, (k + 1) * BLK
        d_ref[...] = w_ref[lo:hi, lo:hi]
        di_ref[...] = eye
        lax.fori_loop(0, BLK // 2, step, 0)
        lkk = dt_ref[...].T
        ikk = di_ref[...]
        l_ref[lo:hi, lo:hi] = lkk
        inv_ref[lo:hi, lo:hi] = ikk
        inv_diag.append(ikk)
        if k + 1 < nb:
            panel = _mm_t(w_ref[hi:, lo:hi], ikk)
            l_ref[hi:, lo:hi] = panel
            w_ref[hi:, hi:] = w_ref[hi:, hi:] - _mm_t(panel, panel)
    for i in range(nb):
        for j in range(i - 1, -1, -1):
            acc = _mm(l_ref[i * BLK:(i + 1) * BLK, j * BLK:i * BLK], inv_ref[j * BLK:i * BLK, j * BLK:(j + 1) * BLK])
            inv_ref[i * BLK:(i + 1) * BLK, j * BLK:(j + 1) * BLK] = -_mm(inv_diag[i], acc)


def factor_and_inverse(sym):
    n = sym.shape[0]
    return pl.pallas_call(
        _factor_kernel,
        out_shape=(jax.ShapeDtypeStruct((n, n), jnp.float32), jax.ShapeDtypeStruct((n, n), jnp.float32)),
        in_specs=[pl.BlockSpec(memory_space=pltpu.VMEM)],
        out_specs=(pl.BlockSpec(memory_space=pltpu.VMEM), pl.BlockSpec(memory_space=pltpu.VMEM)),
        scratch_shapes=[pltpu.VMEM((n, n), jnp.float32)] + [pltpu.VMEM((BLK, BLK), jnp.float32)] * 3,
    )(sym)


def _block_add_kernel(col0, idx_ref, base_ref, add_ref, out_ref, sem):
    width = out_ref.shape[1]
    copy = pltpu.make_async_copy(base_ref.at[:, pl.ds(col0, width)], out_ref, sem)
    copy.start()
    copy.wait()

    def accumulate(i, c):
        r = idx_ref[i]
        out_ref[pl.ds(r, 1), :] = out_ref[pl.ds(r, 1), :] + add_ref[pl.ds(i, 1), :]
        return c

    lax.fori_loop(0, add_ref.shape[0], accumulate, 0)


def add_rows(base, col0, width, rows, values):
    return pl.pallas_call(
        functools.partial(_block_add_kernel, col0),
        out_shape=jax.ShapeDtypeStruct((base.shape[0], width), base.dtype),
        in_specs=[
            pl.BlockSpec(memory_space=pltpu.SMEM),
            pl.BlockSpec(memory_space=pl.ANY),
            pl.BlockSpec(memory_space=pltpu.VMEM),
        ],
        out_specs=pl.BlockSpec(memory_space=pltpu.VMEM),
        scratch_shapes=[pltpu.SemaphoreType.DMA(())],
    )(rows, base, values)


def local(front_block, child_blocks, child_rows, child_dest, panel_owner):
    local_rows = front_block[0]
    front_count = lax.axis_size("front")
    blocks = child_blocks[0, 0]
    row_lists = child_rows[0, 0]
    target_front = child_dest[0, 0, :, 0]
    block_count = target_front.shape[0]
    position = jnp.arange(block_count, dtype=jnp.int32)
    same_front = target_front[:, None] == target_front[None, :]
    earlier = position[None, :] < position[:, None]
    slot_index = target_front * CAP + jnp.sum((same_front & earlier).astype(jnp.int32), axis=1)
    row_lanes = jnp.zeros(blocks.shape[:2] + (128,), jnp.float32).at[:, :, 0].set(row_lists.astype(jnp.float32))
    send_panel = pack_slots(jnp.concatenate([blocks[:, :, :PB], row_lanes], axis=2), slot_index, front_count)
    got_both = lax.all_to_all(send_panel, "front", split_axis=0, concat_axis=0, tiled=True)
    got_panel = got_both[..., :PB]
    flat_rows = got_both[..., PB].reshape(-1).astype(jnp.int32)
    panel_part = add_rows(local_rows, 0, PB, flat_rows, got_panel.reshape(-1, PB))
    send_trail = pack_slots(blocks[:, :, PB:], slot_index, front_count)
    trailing_rows = lax.all_to_all(send_trail, "front", split_axis=0, concat_axis=0, tiled=True)
    win_cols = local_rows.shape[1] - PB
    owner_index = panel_owner[0]
    is_owner = lax.axis_index("grp") == owner_index

    pivot_block = broadcast_from(panel_part[:PB], owner_index, "grp")
    window_rows = broadcast_from(panel_part[PB:PB + win_cols], owner_index, "grp")
    symmetric = 0.5 * (pivot_block + pivot_block.T)
    pivot_factor, factor_inverse = factor_and_inverse(symmetric)
    solved = jnp.dot(panel_part, factor_inverse.T, precision=FAST)
    window = jnp.dot(window_rows, factor_inverse.T, precision=FAST)
    schur_part = local_rows[:, PB:] - jnp.dot(solved, window.T, precision=FAST)
    schur_part = add_rows(schur_part, 0, win_cols, flat_rows, trailing_rows.reshape(-1, win_cols))
    head = jnp.where(is_owner, pivot_factor, solved[:PB])
    panel_rows = lax.dynamic_update_slice(solved, head, (0, 0))
    return (panel_rows[None], schur_part[None])


def solution(mesh):
    placed = (
        P("front", "grp", None),
        P("front", "grp", None, None, None),
        P("front", "grp", None, None),
        P("front", "grp", None, None),
        P("front"),
    )
    return jax.shard_map(
        local,
        mesh=mesh,
        in_specs=placed,
        out_specs=(P("front", "grp", None), P("front", "grp", None)),
        check_vma=False,
    )
```

```python
import functools

import jax
import jax.numpy as jnp
from jax import lax
from jax.experimental import pallas as pl
from jax.experimental.pallas import tpu as pltpu
from jax.sharding import PartitionSpec as P

PB = 512
CAP = 2
BLK = 128
EXACT = lax.Precision.HIGHEST
FAST = lax.Precision.HIGH


def pack_slots(values, slot_index, front_count):
    empty = jnp.zeros((front_count * CAP,) + values.shape[1:], values.dtype)
    filled = empty.at[slot_index].set(values)
    return filled.reshape((front_count, CAP) + values.shape[1:])


def pairs(size, bit):
    return [(d, d ^ bit) for d in range(size)]


def broadcast_from(x, owner, axis):
    size = lax.axis_size(axis)
    me = lax.axis_index(axis)
    got = lax.ppermute(x, axis, pairs(size, 1))
    x = jnp.where(me == owner, x, got)
    half_rows = x.shape[0] // 2
    core = me % 2
    half = jnp.where(core == 0, x[:half_rows], x[half_rows:])
    bit = 2
    while bit < size:
        got = lax.ppermute(half, axis, pairs(size, bit))
        half = jnp.where(me // bit == owner // bit, half, got)
        bit *= 2
    other = lax.ppermute(half, axis, pairs(size, 1))
    return jnp.where(
        core == 0,
        jnp.concatenate([half, other], axis=0),
        jnp.concatenate([other, half], axis=0),
    )


def _mm(a, b):
    return jnp.dot(a, b, precision=EXACT, preferred_element_type=jnp.float32)


def _mm_t(a, b):
    return lax.dot_general(a, b, (((1,), (1,)), ((), ())), precision=EXACT, preferred_element_type=jnp.float32)


def _factor_kernel(s_ref, l_ref, inv_ref, w_ref, d_ref, dt_ref, di_ref):
    n = s_ref.shape[0]
    nb = n // BLK
    w_ref[...] = s_ref[...]
    l_ref[...] = jnp.zeros_like(l_ref)
    inv_ref[...] = jnp.zeros_like(inv_ref)
    sub = lax.broadcasted_iota(jnp.int32, (BLK, BLK), 0)
    lane = lax.broadcasted_iota(jnp.int32, (BLK, BLK), 1)
    lane1 = lax.broadcasted_iota(jnp.int32, (1, BLK), 1)
    sub1 = lax.broadcasted_iota(jnp.int32, (BLK, 1), 0)
    eye = jnp.where(sub == lane, 1.0, 0.0).astype(jnp.float32)

    def step(t, carry):
        j = 2 * t
        r0 = d_ref[pl.ds(j, 1), :]
        r1 = d_ref[pl.ds(j + 1, 1), :]
        d0 = jnp.sum(jnp.where(lane1 == j, r0, 0.0), axis=1, keepdims=True)
        e = jnp.sum(jnp.where(lane1 == j, r1, 0.0), axis=1, keepdims=True)
        d1 = jnp.sum(jnp.where(lane1 == j + 1, r1, 0.0), axis=1, keepdims=True)
        s0 = lax.rsqrt(d0)
        l10 = e * s0
        s1 = lax.rsqrt(d1 - l10 * l10)
        c0 = jnp.where(lane1 >= j, r0 * s0, 0.0)
        c1 = jnp.where(lane1 >= j + 1, (r1 - l10 * c0) * s1, 0.0)
        wv = d_ref[...]
        col0 = jnp.sum(jnp.where(lane == j, wv, 0.0), axis=1, keepdims=True)
        col1 = jnp.sum(jnp.where(lane == j + 1, wv, 0.0), axis=1, keepdims=True)
        ccol0 = jnp.where(sub1 >= j, col0 * s0, 0.0)
        ccol1 = jnp.where(sub1 >= j + 1, (col1 - l10 * ccol0) * s1, 0.0)
        d_ref[...] = wv - ccol0 * c0 - ccol1 * c1
        dt_ref[pl.ds(j, 1), :] = c0
        dt_ref[pl.ds(j + 1, 1), :] = c1
        x0 = di_ref[pl.ds(j, 1), :] * s0
        x1 = (di_ref[pl.ds(j + 1, 1), :] - l10 * x0) * s1
        below = sub1 > j + 1
        di_ref[...] = di_ref[...] - jnp.where(below, ccol0, 0.0) * x0 - jnp.where(below, ccol1, 0.0) * x1
        di_ref[pl.ds(j, 1), :] = x0
        di_ref[pl.ds(j + 1, 1), :] = x1
        return carry

    inv_diag = []
    for k in range(nb):
        lo, hi = k * BLK, (k + 1) * BLK
        d_ref[...] = w_ref[lo:hi, lo:hi]
        di_ref[...] = eye
        lax.fori_loop(0, BLK // 2, step, 0)
        lkk = dt_ref[...].T
        ikk = di_ref[...]
        l_ref[lo:hi, lo:hi] = lkk
        inv_ref[lo:hi, lo:hi] = ikk
        inv_diag.append(ikk)
        if k + 1 < nb:
            panel = _mm_t(w_ref[hi:, lo:hi], ikk)
            l_ref[hi:, lo:hi] = panel
            w_ref[hi:, hi:] = w_ref[hi:, hi:] - _mm_t(panel, panel)
    for i in range(nb):
        for j in range(i - 1, -1, -1):
            acc = _mm(l_ref[i * BLK:(i + 1) * BLK, j * BLK:i * BLK], inv_ref[j * BLK:i * BLK, j * BLK:(j + 1) * BLK])
            inv_ref[i * BLK:(i + 1) * BLK, j * BLK:(j + 1) * BLK] = -_mm(inv_diag[i], acc)


def factor_and_inverse(sym):
    n = sym.shape[0]
    return pl.pallas_call(
        _factor_kernel,
        out_shape=(jax.ShapeDtypeStruct((n, n), jnp.float32), jax.ShapeDtypeStruct((n, n), jnp.float32)),
        in_specs=[pl.BlockSpec(memory_space=pltpu.VMEM)],
        out_specs=(pl.BlockSpec(memory_space=pltpu.VMEM), pl.BlockSpec(memory_space=pltpu.VMEM)),
        scratch_shapes=[pltpu.VMEM((n, n), jnp.float32)] + [pltpu.VMEM((BLK, BLK), jnp.float32)] * 3,
    )(sym)


def _block_add_kernel(col0, idx_ref, base_ref, add_ref, out_ref, sem):
    width = out_ref.shape[1]
    copy = pltpu.make_async_copy(base_ref.at[:, pl.ds(col0, width)], out_ref, sem)
    copy.start()
    copy.wait()

    def accumulate(i, c):
        r = idx_ref[i]
        out_ref[pl.ds(r, 1), :] = out_ref[pl.ds(r, 1), :] + add_ref[pl.ds(i, 1), :]
        return c

    lax.fori_loop(0, add_ref.shape[0], accumulate, 0)


def add_rows(base, col0, width, rows, values):
    return pl.pallas_call(
        functools.partial(_block_add_kernel, col0),
        out_shape=jax.ShapeDtypeStruct((base.shape[0], width), base.dtype),
        in_specs=[
            pl.BlockSpec(memory_space=pltpu.SMEM),
            pl.BlockSpec(memory_space=pl.ANY),
            pl.BlockSpec(memory_space=pltpu.VMEM),
        ],
        out_specs=pl.BlockSpec(memory_space=pltpu.VMEM),
        scratch_shapes=[pltpu.SemaphoreType.DMA(())],
    )(rows, base, values)


def exchange(send, axis):
    size = lax.axis_size(axis)
    me = lax.axis_index(axis)
    got = [lax.dynamic_index_in_dim(send, me, axis=0, keepdims=False)]
    for shift in range(1, size):
        outgoing = lax.dynamic_index_in_dim(send, (me + shift) % size, axis=0, keepdims=False)
        got.append(lax.ppermute(outgoing, axis, [(d, (d + shift) % size) for d in range(size)]))
    by_shift = jnp.stack(got, axis=0)
    return jnp.take(by_shift, (me - jnp.arange(size)) % size, axis=0)


def local(front_block, child_blocks, child_rows, child_dest, panel_owner):
    local_rows = front_block[0]
    front_count = lax.axis_size("front")
    blocks = child_blocks[0, 0]
    row_lists = child_rows[0, 0]
    target_front = child_dest[0, 0, :, 0]
    block_count = target_front.shape[0]
    position = jnp.arange(block_count, dtype=jnp.int32)
    same_front = target_front[:, None] == target_front[None, :]
    earlier = position[None, :] < position[:, None]
    slot_index = target_front * CAP + jnp.sum((same_front & earlier).astype(jnp.int32), axis=1)
    row_lanes = jnp.zeros(blocks.shape[:2] + (128,), jnp.float32).at[:, :, 0].set(row_lists.astype(jnp.float32))
    send_panel = pack_slots(jnp.concatenate([blocks[:, :, :PB], row_lanes], axis=2), slot_index, front_count)
    got_both = exchange(send_panel, "front")
    got_panel = got_both[..., :PB]
    flat_rows = got_both[..., PB].reshape(-1).astype(jnp.int32)
    panel_part = add_rows(local_rows, 0, PB, flat_rows, got_panel.reshape(-1, PB))
    send_trail = pack_slots(blocks[:, :, PB:], slot_index, front_count)
    trailing_rows = lax.all_to_all(send_trail, "front", split_axis=0, concat_axis=0, tiled=True)
    win_cols = local_rows.shape[1] - PB
    owner_index = panel_owner[0]
    is_owner = lax.axis_index("grp") == owner_index

    pivot_block = broadcast_from(panel_part[:PB], owner_index, "grp")
    window_rows = broadcast_from(panel_part[PB:PB + win_cols], owner_index, "grp")
    symmetric = 0.5 * (pivot_block + pivot_block.T)
    pivot_factor, factor_inverse = factor_and_inverse(symmetric)
    solved = jnp.dot(panel_part, factor_inverse.T, precision=FAST)
    window = jnp.dot(window_rows, factor_inverse.T, precision=FAST)
    schur_part = local_rows[:, PB:] - jnp.dot(solved, window.T, precision=FAST)
    schur_part = add_rows(schur_part, 0, win_cols, flat_rows, trailing_rows.reshape(-1, win_cols))
    head = jnp.where(is_owner, pivot_factor, solved[:PB])
    panel_rows = lax.dynamic_update_slice(solved, head, (0, 0))
    return (panel_rows[None], schur_part[None])


def solution(mesh):
    placed = (
        P("front", "grp", None),
        P("front", "grp", None, None, None),
        P("front", "grp", None, None),
        P("front", "grp", None, None),
        P("front"),
    )
    return jax.shard_map(
        local,
        mesh=mesh,
        in_specs=placed,
        out_specs=(P("front", "grp", None), P("front", "grp", None)),
        check_vma=False,
    )
```

```python
import functools

import jax
import jax.numpy as jnp
from jax import lax
from jax.experimental import pallas as pl
from jax.experimental.pallas import tpu as pltpu
from jax.sharding import PartitionSpec as P

PB = 512
CAP = 2
BLK = 128
EXACT = lax.Precision.HIGHEST
FAST = lax.Precision.HIGH


def pack_slots(values, slot_index, front_count):
    empty = jnp.zeros((front_count * CAP,) + values.shape[1:], values.dtype)
    filled = empty.at[slot_index].set(values)
    return filled.reshape((front_count, CAP) + values.shape[1:])


def pairs(size, bit):
    return [(d, d ^ bit) for d in range(size)]


def broadcast_from(x, owner, axis):
    size = lax.axis_size(axis)
    me = lax.axis_index(axis)
    got = lax.ppermute(x, axis, pairs(size, 1))
    x = jnp.where(me == owner, x, got)
    half_rows = x.shape[0] // 2
    core = me % 2
    half = jnp.where(core == 0, x[:half_rows], x[half_rows:])
    bit = 2
    while bit < size:
        got = lax.ppermute(half, axis, pairs(size, bit))
        half = jnp.where(me // bit == owner // bit, half, got)
        bit *= 2
    other = lax.ppermute(half, axis, pairs(size, 1))
    return jnp.where(
        core == 0,
        jnp.concatenate([half, other], axis=0),
        jnp.concatenate([other, half], axis=0),
    )


def _mm(a, b):
    return jnp.dot(a, b, precision=EXACT, preferred_element_type=jnp.float32)


def _mm_t(a, b):
    return lax.dot_general(a, b, (((1,), (1,)), ((), ())), precision=EXACT, preferred_element_type=jnp.float32)


def _factor_kernel(s_ref, l_ref, inv_ref, w_ref, d_ref, dt_ref, di_ref):
    n = s_ref.shape[0]
    nb = n // BLK
    w_ref[...] = s_ref[...]
    l_ref[...] = jnp.zeros_like(l_ref)
    inv_ref[...] = jnp.zeros_like(inv_ref)
    sub = lax.broadcasted_iota(jnp.int32, (BLK, BLK), 0)
    lane = lax.broadcasted_iota(jnp.int32, (BLK, BLK), 1)
    lane1 = lax.broadcasted_iota(jnp.int32, (1, BLK), 1)
    sub1 = lax.broadcasted_iota(jnp.int32, (BLK, 1), 0)
    eye = jnp.where(sub == lane, 1.0, 0.0).astype(jnp.float32)

    def step(t, carry):
        j = 2 * t
        r0 = d_ref[pl.ds(j, 1), :]
        r1 = d_ref[pl.ds(j + 1, 1), :]
        d0 = jnp.sum(jnp.where(lane1 == j, r0, 0.0), axis=1, keepdims=True)
        e = jnp.sum(jnp.where(lane1 == j, r1, 0.0), axis=1, keepdims=True)
        d1 = jnp.sum(jnp.where(lane1 == j + 1, r1, 0.0), axis=1, keepdims=True)
        s0 = lax.rsqrt(d0)
        l10 = e * s0
        s1 = lax.rsqrt(d1 - l10 * l10)
        c0 = jnp.where(lane1 >= j, r0 * s0, 0.0)
        c1 = jnp.where(lane1 >= j + 1, (r1 - l10 * c0) * s1, 0.0)
        wv = d_ref[...]
        col0 = jnp.sum(jnp.where(lane == j, wv, 0.0), axis=1, keepdims=True)
        col1 = jnp.sum(jnp.where(lane == j + 1, wv, 0.0), axis=1, keepdims=True)
        ccol0 = jnp.where(sub1 >= j, col0 * s0, 0.0)
        ccol1 = jnp.where(sub1 >= j + 1, (col1 - l10 * ccol0) * s1, 0.0)
        d_ref[...] = wv - ccol0 * c0 - ccol1 * c1
        dt_ref[pl.ds(j, 1), :] = c0
        dt_ref[pl.ds(j + 1, 1), :] = c1
        x0 = di_ref[pl.ds(j, 1), :] * s0
        x1 = (di_ref[pl.ds(j + 1, 1), :] - l10 * x0) * s1
        below = sub1 > j + 1
        di_ref[...] = di_ref[...] - jnp.where(below, ccol0, 0.0) * x0 - jnp.where(below, ccol1, 0.0) * x1
        di_ref[pl.ds(j, 1), :] = x0
        di_ref[pl.ds(j + 1, 1), :] = x1
        return carry

    inv_diag = []
    for k in range(nb):
        lo, hi = k * BLK, (k + 1) * BLK
        d_ref[...] = w_ref[lo:hi, lo:hi]
        di_ref[...] = eye
        lax.fori_loop(0, BLK // 2, step, 0)
        lkk = dt_ref[...].T
        ikk = di_ref[...]
        l_ref[lo:hi, lo:hi] = lkk
        inv_ref[lo:hi, lo:hi] = ikk
        inv_diag.append(ikk)
        if k + 1 < nb:
            panel = _mm_t(w_ref[hi:, lo:hi], ikk)
            l_ref[hi:, lo:hi] = panel
            w_ref[hi:, hi:] = w_ref[hi:, hi:] - _mm_t(panel, panel)
    for i in range(nb):
        for j in range(i - 1, -1, -1):
            acc = _mm(l_ref[i * BLK:(i + 1) * BLK, j * BLK:i * BLK], inv_ref[j * BLK:i * BLK, j * BLK:(j + 1) * BLK])
            inv_ref[i * BLK:(i + 1) * BLK, j * BLK:(j + 1) * BLK] = -_mm(inv_diag[i], acc)


def factor_and_inverse(sym):
    n = sym.shape[0]
    return pl.pallas_call(
        _factor_kernel,
        out_shape=(jax.ShapeDtypeStruct((n, n), jnp.float32), jax.ShapeDtypeStruct((n, n), jnp.float32)),
        in_specs=[pl.BlockSpec(memory_space=pltpu.VMEM)],
        out_specs=(pl.BlockSpec(memory_space=pltpu.VMEM), pl.BlockSpec(memory_space=pltpu.VMEM)),
        scratch_shapes=[pltpu.VMEM((n, n), jnp.float32)] + [pltpu.VMEM((BLK, BLK), jnp.float32)] * 3,
    )(sym)


def _block_add_kernel(col0, idx_ref, base_ref, add_ref, out_ref, sem):
    width = out_ref.shape[1]
    copy = pltpu.make_async_copy(base_ref.at[:, pl.ds(col0, width)], out_ref, sem)
    copy.start()
    copy.wait()

    def accumulate(i, c):
        r = idx_ref[i]
        out_ref[pl.ds(r, 1), :] = out_ref[pl.ds(r, 1), :] + add_ref[pl.ds(i, 1), :]
        return c

    lax.fori_loop(0, add_ref.shape[0], accumulate, 0)


def add_rows(base, col0, width, rows, values):
    return pl.pallas_call(
        functools.partial(_block_add_kernel, col0),
        out_shape=jax.ShapeDtypeStruct((base.shape[0], width), base.dtype),
        in_specs=[
            pl.BlockSpec(memory_space=pltpu.SMEM),
            pl.BlockSpec(memory_space=pl.ANY),
            pl.BlockSpec(memory_space=pltpu.VMEM),
        ],
        out_specs=pl.BlockSpec(memory_space=pltpu.VMEM),
        scratch_shapes=[pltpu.SemaphoreType.DMA(())],
    )(rows, base, values)


def _head_kernel(flag_ref, factor_ref, solved_ref, out_ref, sem):
    @pl.when(flag_ref[0] == 1)
    def _():
        copy = pltpu.make_async_copy(factor_ref, out_ref.at[pl.ds(0, factor_ref.shape[0])], sem)
        copy.start()
        copy.wait()


def put_head(solved, factor, flag):
    return pl.pallas_call(
        _head_kernel,
        out_shape=jax.ShapeDtypeStruct(solved.shape, solved.dtype),
        in_specs=[
            pl.BlockSpec(memory_space=pltpu.SMEM),
            pl.BlockSpec(memory_space=pltpu.VMEM),
            pl.BlockSpec(memory_space=pl.ANY),
        ],
        out_specs=pl.BlockSpec(memory_space=pl.ANY),
        scratch_shapes=[pltpu.SemaphoreType.DMA(())],
        input_output_aliases={2: 0},
    )(flag, factor, solved)


def local(front_block, child_blocks, child_rows, child_dest, panel_owner):
    local_rows = front_block[0]
    front_count = lax.axis_size("front")
    blocks = child_blocks[0, 0]
    row_lists = child_rows[0, 0]
    target_front = child_dest[0, 0, :, 0]
    block_count = target_front.shape[0]
    position = jnp.arange(block_count, dtype=jnp.int32)
    same_front = target_front[:, None] == target_front[None, :]
    earlier = position[None, :] < position[:, None]
    slot_index = target_front * CAP + jnp.sum((same_front & earlier).astype(jnp.int32), axis=1)
    row_lanes = jnp.zeros(blocks.shape[:2] + (128,), jnp.float32).at[:, :, 0].set(row_lists.astype(jnp.float32))
    send_panel = pack_slots(jnp.concatenate([blocks[:, :, :PB], row_lanes], axis=2), slot_index, front_count)
    got_both = lax.all_to_all(send_panel, "front", split_axis=0, concat_axis=0, tiled=True)
    got_panel = got_both[..., :PB]
    flat_rows = got_both[..., PB].reshape(-1).astype(jnp.int32)
    panel_part = add_rows(local_rows, 0, PB, flat_rows, got_panel.reshape(-1, PB))
    send_trail = pack_slots(blocks[:, :, PB:], slot_index, front_count)
    trailing_rows = lax.all_to_all(send_trail, "front", split_axis=0, concat_axis=0, tiled=True)
    win_cols = local_rows.shape[1] - PB
    owner_index = panel_owner[0]
    is_owner = lax.axis_index("grp") == owner_index

    pivot_block = broadcast_from(panel_part[:PB], owner_index, "grp")
    window_rows = broadcast_from(panel_part[PB:PB + win_cols], owner_index, "grp")
    symmetric = 0.5 * (pivot_block + pivot_block.T)
    pivot_factor, factor_inverse = factor_and_inverse(symmetric)
    solved = jnp.dot(panel_part, factor_inverse.T, precision=FAST)
    window = jnp.dot(window_rows, factor_inverse.T, precision=FAST)
    schur_part = local_rows[:, PB:] - jnp.dot(solved, window.T, precision=FAST)
    schur_part = add_rows(schur_part, 0, win_cols, flat_rows, trailing_rows.reshape(-1, win_cols))
    panel_rows = put_head(solved, pivot_factor, is_owner.astype(jnp.int32).reshape(1))
    return (panel_rows[None], schur_part[None])


def solution(mesh):
    placed = (
        P("front", "grp", None),
        P("front", "grp", None, None, None),
        P("front", "grp", None, None),
        P("front", "grp", None, None),
        P("front"),
    )
    return jax.shard_map(
        local,
        mesh=mesh,
        in_specs=placed,
        out_specs=(P("front", "grp", None), P("front", "grp", None)),
        check_vma=False,
    )
```

```python
import functools

import jax
import jax.numpy as jnp
from jax import lax
from jax.experimental import pallas as pl
from jax.experimental.pallas import tpu as pltpu
from jax.sharding import PartitionSpec as P

PB = 512
CAP = 2
BLK = 128
EXACT = lax.Precision.HIGHEST
FAST = lax.Precision.HIGH


def pack_slots(values, slot_index, front_count):
    empty = jnp.zeros((front_count * CAP,) + values.shape[1:], values.dtype)
    filled = empty.at[slot_index].set(values)
    return filled.reshape((front_count, CAP) + values.shape[1:])


def pairs(size, bit):
    return [(d, d ^ bit) for d in range(size)]


def broadcast_from(x, owner, axis):
    size = lax.axis_size(axis)
    me = lax.axis_index(axis)
    got = lax.ppermute(x, axis, pairs(size, 1))
    x = jnp.where(me == owner, x, got)
    half_rows = x.shape[0] // 2
    core = me % 2
    half = jnp.where(core == 0, x[:half_rows], x[half_rows:])
    bit = 2
    while bit < size:
        got = lax.ppermute(half, axis, pairs(size, bit))
        half = jnp.where(me // bit == owner // bit, half, got)
        bit *= 2
    other = lax.ppermute(half, axis, pairs(size, 1))
    return jnp.where(
        core == 0,
        jnp.concatenate([half, other], axis=0),
        jnp.concatenate([other, half], axis=0),
    )


def broadcast_whole(x, owner, axis):
    size = lax.axis_size(axis)
    me = lax.axis_index(axis)
    bit = 1
    while bit < size:
        got = lax.ppermute(x, axis, pairs(size, bit))
        x = jnp.where(me // bit == owner // bit, x, got)
        bit *= 2
    return x


def _mm(a, b):
    return jnp.dot(a, b, precision=EXACT, preferred_element_type=jnp.float32)


def _mm_t(a, b):
    return lax.dot_general(a, b, (((1,), (1,)), ((), ())), precision=EXACT, preferred_element_type=jnp.float32)


def _factor_kernel(s_ref, l_ref, inv_ref, w_ref, d_ref, dt_ref, di_ref):
    n = s_ref.shape[0]
    nb = n // BLK
    w_ref[...] = s_ref[...]
    l_ref[...] = jnp.zeros_like(l_ref)
    inv_ref[...] = jnp.zeros_like(inv_ref)
    sub = lax.broadcasted_iota(jnp.int32, (BLK, BLK), 0)
    lane = lax.broadcasted_iota(jnp.int32, (BLK, BLK), 1)
    lane1 = lax.broadcasted_iota(jnp.int32, (1, BLK), 1)
    sub1 = lax.broadcasted_iota(jnp.int32, (BLK, 1), 0)
    eye = jnp.where(sub == lane, 1.0, 0.0).astype(jnp.float32)

    def step(t, carry):
        j = 2 * t
        r0 = d_ref[pl.ds(j, 1), :]
        r1 = d_ref[pl.ds(j + 1, 1), :]
        d0 = jnp.sum(jnp.where(lane1 == j, r0, 0.0), axis=1, keepdims=True)
        e = jnp.sum(jnp.where(lane1 == j, r1, 0.0), axis=1, keepdims=True)
        d1 = jnp.sum(jnp.where(lane1 == j + 1, r1, 0.0), axis=1, keepdims=True)
        s0 = lax.rsqrt(d0)
        l10 = e * s0
        s1 = lax.rsqrt(d1 - l10 * l10)
        c0 = jnp.where(lane1 >= j, r0 * s0, 0.0)
        c1 = jnp.where(lane1 >= j + 1, (r1 - l10 * c0) * s1, 0.0)
        wv = d_ref[...]
        col0 = jnp.sum(jnp.where(lane == j, wv, 0.0), axis=1, keepdims=True)
        col1 = jnp.sum(jnp.where(lane == j + 1, wv, 0.0), axis=1, keepdims=True)
        ccol0 = jnp.where(sub1 >= j, col0 * s0, 0.0)
        ccol1 = jnp.where(sub1 >= j + 1, (col1 - l10 * ccol0) * s1, 0.0)
        d_ref[...] = wv - ccol0 * c0 - ccol1 * c1
        dt_ref[pl.ds(j, 1), :] = c0
        dt_ref[pl.ds(j + 1, 1), :] = c1
        x0 = di_ref[pl.ds(j, 1), :] * s0
        x1 = (di_ref[pl.ds(j + 1, 1), :] - l10 * x0) * s1
        below = sub1 > j + 1
        di_ref[...] = di_ref[...] - jnp.where(below, ccol0, 0.0) * x0 - jnp.where(below, ccol1, 0.0) * x1
        di_ref[pl.ds(j, 1), :] = x0
        di_ref[pl.ds(j + 1, 1), :] = x1
        return carry

    inv_diag = []
    for k in range(nb):
        lo, hi = k * BLK, (k + 1) * BLK
        d_ref[...] = w_ref[lo:hi, lo:hi]
        di_ref[...] = eye
        lax.fori_loop(0, BLK // 2, step, 0)
        lkk = dt_ref[...].T
        ikk = di_ref[...]
        l_ref[lo:hi, lo:hi] = lkk
        inv_ref[lo:hi, lo:hi] = ikk
        inv_diag.append(ikk)
        if k + 1 < nb:
            panel = _mm_t(w_ref[hi:, lo:hi], ikk)
            l_ref[hi:, lo:hi] = panel
            w_ref[hi:, hi:] = w_ref[hi:, hi:] - _mm_t(panel, panel)
    for i in range(nb):
        for j in range(i - 1, -1, -1):
            acc = _mm(l_ref[i * BLK:(i + 1) * BLK, j * BLK:i * BLK], inv_ref[j * BLK:i * BLK, j * BLK:(j + 1) * BLK])
            inv_ref[i * BLK:(i + 1) * BLK, j * BLK:(j + 1) * BLK] = -_mm(inv_diag[i], acc)


def factor_and_inverse(sym):
    n = sym.shape[0]
    return pl.pallas_call(
        _factor_kernel,
        out_shape=(jax.ShapeDtypeStruct((n, n), jnp.float32), jax.ShapeDtypeStruct((n, n), jnp.float32)),
        in_specs=[pl.BlockSpec(memory_space=pltpu.VMEM)],
        out_specs=(pl.BlockSpec(memory_space=pltpu.VMEM), pl.BlockSpec(memory_space=pltpu.VMEM)),
        scratch_shapes=[pltpu.VMEM((n, n), jnp.float32)] + [pltpu.VMEM((BLK, BLK), jnp.float32)] * 3,
    )(sym)


def _block_add_kernel(col0, idx_ref, base_ref, add_ref, out_ref, sem):
    width = out_ref.shape[1]
    copy = pltpu.make_async_copy(base_ref.at[:, pl.ds(col0, width)], out_ref, sem)
    copy.start()
    copy.wait()

    def accumulate(i, c):
        r = idx_ref[i]
        out_ref[pl.ds(r, 1), :] = out_ref[pl.ds(r, 1), :] + add_ref[pl.ds(i, 1), :]
        return c

    lax.fori_loop(0, add_ref.shape[0], accumulate, 0)


def add_rows(base, col0, width, rows, values):
    return pl.pallas_call(
        functools.partial(_block_add_kernel, col0),
        out_shape=jax.ShapeDtypeStruct((base.shape[0], width), base.dtype),
        in_specs=[
            pl.BlockSpec(memory_space=pltpu.SMEM),
            pl.BlockSpec(memory_space=pl.ANY),
            pl.BlockSpec(memory_space=pltpu.VMEM),
        ],
        out_specs=pl.BlockSpec(memory_space=pltpu.VMEM),
        scratch_shapes=[pltpu.SemaphoreType.DMA(())],
    )(rows, base, values)


def _head_kernel(flag_ref, factor_ref, solved_ref, out_ref, sem):
    @pl.when(flag_ref[0] == 1)
    def _():
        copy = pltpu.make_async_copy(factor_ref, out_ref.at[pl.ds(0, factor_ref.shape[0])], sem)
        copy.start()
        copy.wait()


def put_head(solved, factor, flag):
    return pl.pallas_call(
        _head_kernel,
        out_shape=jax.ShapeDtypeStruct(solved.shape, solved.dtype),
        in_specs=[
            pl.BlockSpec(memory_space=pltpu.SMEM),
            pl.BlockSpec(memory_space=pltpu.VMEM),
            pl.BlockSpec(memory_space=pl.ANY),
        ],
        out_specs=pl.BlockSpec(memory_space=pl.ANY),
        scratch_shapes=[pltpu.SemaphoreType.DMA(())],
        input_output_aliases={2: 0},
    )(flag, factor, solved)


def local(front_block, child_blocks, child_rows, child_dest, panel_owner):
    local_rows = front_block[0]
    front_count = lax.axis_size("front")
    blocks = child_blocks[0, 0]
    row_lists = child_rows[0, 0]
    target_front = child_dest[0, 0, :, 0]
    block_count = target_front.shape[0]
    position = jnp.arange(block_count, dtype=jnp.int32)
    same_front = target_front[:, None] == target_front[None, :]
    earlier = position[None, :] < position[:, None]
    slot_index = target_front * CAP + jnp.sum((same_front & earlier).astype(jnp.int32), axis=1)
    row_lanes = jnp.zeros(blocks.shape[:2] + (128,), jnp.float32).at[:, :, 0].set(row_lists.astype(jnp.float32))
    send_panel = pack_slots(jnp.concatenate([blocks[:, :, :PB], row_lanes], axis=2), slot_index, front_count)
    got_both = lax.all_to_all(send_panel, "front", split_axis=0, concat_axis=0, tiled=True)
    got_panel = got_both[..., :PB]
    flat_rows = got_both[..., PB].reshape(-1).astype(jnp.int32)
    panel_part = add_rows(local_rows, 0, PB, flat_rows, got_panel.reshape(-1, PB))
    send_trail = pack_slots(blocks[:, :, PB:], slot_index, front_count)
    trailing_rows = lax.all_to_all(send_trail, "front", split_axis=0, concat_axis=0, tiled=True)
    win_cols = local_rows.shape[1] - PB
    owner_index = panel_owner[0]
    is_owner = lax.axis_index("grp") == owner_index

    pivot_block = broadcast_from(panel_part[:PB], owner_index, "grp")
    window_rows = broadcast_whole(panel_part[PB:PB + win_cols], owner_index, "grp")
    symmetric = 0.5 * (pivot_block + pivot_block.T)
    pivot_factor, factor_inverse = factor_and_inverse(symmetric)
    solved = jnp.dot(panel_part, factor_inverse.T, precision=FAST)
    window = jnp.dot(window_rows, factor_inverse.T, precision=FAST)
    schur_part = local_rows[:, PB:] - jnp.dot(solved, window.T, precision=FAST)
    schur_part = add_rows(schur_part, 0, win_cols, flat_rows, trailing_rows.reshape(-1, win_cols))
    panel_rows = put_head(solved, pivot_factor, is_owner.astype(jnp.int32).reshape(1))
    return (panel_rows[None], schur_part[None])


def solution(mesh):
    placed = (
        P("front", "grp", None),
        P("front", "grp", None, None, None),
        P("front", "grp", None, None),
        P("front", "grp", None, None),
        P("front"),
    )
    return jax.shard_map(
        local,
        mesh=mesh,
        in_specs=placed,
        out_specs=(P("front", "grp", None), P("front", "grp", None)),
        check_vma=False,
    )
```

```python
import functools

import jax
import jax.numpy as jnp
from jax import lax
from jax.experimental import pallas as pl
from jax.experimental.pallas import tpu as pltpu
from jax.sharding import PartitionSpec as P

PB = 512
CAP = 2
BLK = 128
EXACT = lax.Precision.HIGHEST
FAST = lax.Precision.HIGH


def pack_slots(values, slot_index, front_count):
    empty = jnp.zeros((front_count * CAP,) + values.shape[1:], values.dtype)
    filled = empty.at[slot_index].set(values)
    return filled.reshape((front_count, CAP) + values.shape[1:])


def pairs(size, bit):
    return [(d, d ^ bit) for d in range(size)]


def broadcast_from(x, owner, axis):
    size = lax.axis_size(axis)
    me = lax.axis_index(axis)
    got = lax.ppermute(x, axis, pairs(size, 1))
    x = jnp.where(me == owner, x, got)
    half_rows = x.shape[0] // 2
    core = me % 2
    half = jnp.where(core == 0, x[:half_rows], x[half_rows:])
    bit = 2
    while bit < size:
        got = lax.ppermute(half, axis, pairs(size, bit))
        half = jnp.where(me // bit == owner // bit, half, got)
        bit *= 2
    other = lax.ppermute(half, axis, pairs(size, 1))
    return jnp.where(
        core == 0,
        jnp.concatenate([half, other], axis=0),
        jnp.concatenate([other, half], axis=0),
    )


def broadcast_whole(x, owner, axis):
    size = lax.axis_size(axis)
    me = lax.axis_index(axis)
    bit = 1
    while bit < size:
        got = lax.ppermute(x, axis, pairs(size, bit))
        x = jnp.where(me // bit == owner // bit, x, got)
        bit *= 2
    return x


def _mm(a, b):
    return jnp.dot(a, b, precision=EXACT, preferred_element_type=jnp.float32)


def _mm_t(a, b):
    return lax.dot_general(a, b, (((1,), (1,)), ((), ())), precision=EXACT, preferred_element_type=jnp.float32)


def _factor_kernel(s_ref, l_ref, inv_ref, w_ref, d_ref, dt_ref, di_ref):
    n = s_ref.shape[0]
    nb = n // BLK
    w_ref[...] = s_ref[...]
    l_ref[...] = jnp.zeros_like(l_ref)
    inv_ref[...] = jnp.zeros_like(inv_ref)
    sub = lax.broadcasted_iota(jnp.int32, (BLK, BLK), 0)
    lane = lax.broadcasted_iota(jnp.int32, (BLK, BLK), 1)
    lane1 = lax.broadcasted_iota(jnp.int32, (1, BLK), 1)
    sub1 = lax.broadcasted_iota(jnp.int32, (BLK, 1), 0)
    eye = jnp.where(sub == lane, 1.0, 0.0).astype(jnp.float32)

    def step(t, carry):
        j = 2 * t
        r0 = d_ref[pl.ds(j, 1), :]
        r1 = d_ref[pl.ds(j + 1, 1), :]
        d0 = jnp.sum(jnp.where(lane1 == j, r0, 0.0), axis=1, keepdims=True)
        e = jnp.sum(jnp.where(lane1 == j, r1, 0.0), axis=1, keepdims=True)
        d1 = jnp.sum(jnp.where(lane1 == j + 1, r1, 0.0), axis=1, keepdims=True)
        s0 = lax.rsqrt(d0)
        l10 = e * s0
        s1 = lax.rsqrt(d1 - l10 * l10)
        c0 = jnp.where(lane1 >= j, r0 * s0, 0.0)
        c1 = jnp.where(lane1 >= j + 1, (r1 - l10 * c0) * s1, 0.0)
        wv = d_ref[...]
        col0 = jnp.sum(jnp.where(lane == j, wv, 0.0), axis=1, keepdims=True)
        col1 = jnp.sum(jnp.where(lane == j + 1, wv, 0.0), axis=1, keepdims=True)
        ccol0 = jnp.where(sub1 >= j, col0 * s0, 0.0)
        ccol1 = jnp.where(sub1 >= j + 1, (col1 - l10 * ccol0) * s1, 0.0)
        d_ref[...] = wv - ccol0 * c0 - ccol1 * c1
        dt_ref[pl.ds(j, 1), :] = c0
        dt_ref[pl.ds(j + 1, 1), :] = c1
        x0 = di_ref[pl.ds(j, 1), :] * s0
        x1 = (di_ref[pl.ds(j + 1, 1), :] - l10 * x0) * s1
        below = sub1 > j + 1
        di_ref[...] = di_ref[...] - jnp.where(below, ccol0, 0.0) * x0 - jnp.where(below, ccol1, 0.0) * x1
        di_ref[pl.ds(j, 1), :] = x0
        di_ref[pl.ds(j + 1, 1), :] = x1
        return carry

    inv_diag = []
    for k in range(nb):
        lo, hi = k * BLK, (k + 1) * BLK
        d_ref[...] = w_ref[lo:hi, lo:hi]
        di_ref[...] = eye
        lax.fori_loop(0, BLK // 2, step, 0)
        lkk = dt_ref[...].T
        ikk = di_ref[...]
        l_ref[lo:hi, lo:hi] = lkk
        inv_ref[lo:hi, lo:hi] = ikk
        inv_diag.append(ikk)
        if k + 1 < nb:
            panel = _mm_t(w_ref[hi:, lo:hi], ikk)
            l_ref[hi:, lo:hi] = panel
            w_ref[hi:, hi:] = w_ref[hi:, hi:] - _mm_t(panel, panel)
    for i in range(nb):
        for j in range(i - 1, -1, -1):
            acc = _mm(l_ref[i * BLK:(i + 1) * BLK, j * BLK:i * BLK], inv_ref[j * BLK:i * BLK, j * BLK:(j + 1) * BLK])
            inv_ref[i * BLK:(i + 1) * BLK, j * BLK:(j + 1) * BLK] = -_mm(inv_diag[i], acc)


def factor_and_inverse(sym):
    n = sym.shape[0]
    return pl.pallas_call(
        _factor_kernel,
        out_shape=(jax.ShapeDtypeStruct((n, n), jnp.float32), jax.ShapeDtypeStruct((n, n), jnp.float32)),
        in_specs=[pl.BlockSpec(memory_space=pltpu.VMEM)],
        out_specs=(pl.BlockSpec(memory_space=pltpu.VMEM), pl.BlockSpec(memory_space=pltpu.VMEM)),
        scratch_shapes=[pltpu.VMEM((n, n), jnp.float32)] + [pltpu.VMEM((BLK, BLK), jnp.float32)] * 3,
    )(sym)


def _block_add_kernel(col0, idx_ref, base_ref, add_ref, out_ref, sem):
    count, width = out_ref.shape
    copy = pltpu.make_async_copy(base_ref.at[pl.ds(0, count), pl.ds(col0, width)], out_ref, sem)
    copy.start()
    copy.wait()

    def accumulate(i, c):
        r = idx_ref[i]

        @pl.when(r < count)
        def _():
            out_ref[pl.ds(r, 1), :] = out_ref[pl.ds(r, 1), :] + add_ref[pl.ds(i, 1), :]

        return c

    lax.fori_loop(0, add_ref.shape[0], accumulate, 0)


def add_rows(base, col0, width, rows, values, count=None):
    count = base.shape[0] if count is None else count
    return pl.pallas_call(
        functools.partial(_block_add_kernel, col0),
        out_shape=jax.ShapeDtypeStruct((count, width), base.dtype),
        in_specs=[
            pl.BlockSpec(memory_space=pltpu.SMEM),
            pl.BlockSpec(memory_space=pl.ANY),
            pl.BlockSpec(memory_space=pltpu.VMEM),
        ],
        out_specs=pl.BlockSpec(memory_space=pltpu.VMEM),
        scratch_shapes=[pltpu.SemaphoreType.DMA(())],
    )(rows, base, values)


def _head_kernel(flag_ref, factor_ref, solved_ref, out_ref, sem):
    @pl.when(flag_ref[0] == 1)
    def _():
        copy = pltpu.make_async_copy(factor_ref, out_ref.at[pl.ds(0, factor_ref.shape[0])], sem)
        copy.start()
        copy.wait()


def put_head(solved, factor, flag):
    return pl.pallas_call(
        _head_kernel,
        out_shape=jax.ShapeDtypeStruct(solved.shape, solved.dtype),
        in_specs=[
            pl.BlockSpec(memory_space=pltpu.SMEM),
            pl.BlockSpec(memory_space=pltpu.VMEM),
            pl.BlockSpec(memory_space=pl.ANY),
        ],
        out_specs=pl.BlockSpec(memory_space=pl.ANY),
        scratch_shapes=[pltpu.SemaphoreType.DMA(())],
        input_output_aliases={2: 0},
    )(flag, factor, solved)


def local(front_block, child_blocks, child_rows, child_dest, panel_owner):
    local_rows = front_block[0]
    front_count = lax.axis_size("front")
    blocks = child_blocks[0, 0]
    row_lists = child_rows[0, 0]
    target_front = child_dest[0, 0, :, 0]
    block_count = target_front.shape[0]
    position = jnp.arange(block_count, dtype=jnp.int32)
    same_front = target_front[:, None] == target_front[None, :]
    earlier = position[None, :] < position[:, None]
    slot_index = target_front * CAP + jnp.sum((same_front & earlier).astype(jnp.int32), axis=1)
    row_lanes = jnp.zeros(blocks.shape[:2] + (128,), jnp.float32).at[:, :, 0].set(row_lists.astype(jnp.float32))
    send_panel = pack_slots(jnp.concatenate([blocks[:, :, :PB], row_lanes], axis=2), slot_index, front_count)
    got_both = lax.all_to_all(send_panel, "front", split_axis=0, concat_axis=0, tiled=True)
    got_panel = got_both[..., :PB]
    flat_rows = got_both[..., PB].reshape(-1).astype(jnp.int32)
    panel_part = add_rows(local_rows, 0, PB, flat_rows, got_panel.reshape(-1, PB))
    send_trail = pack_slots(blocks[:, :, PB:], slot_index, front_count)
    trailing_rows = lax.all_to_all(send_trail, "front", split_axis=0, concat_axis=0, tiled=True)
    win_cols = local_rows.shape[1] - PB
    owner_index = panel_owner[0]
    is_owner = lax.axis_index("grp") == owner_index

    top_rows = add_rows(local_rows, 0, PB, flat_rows, got_panel.reshape(-1, PB), count=PB + win_cols)
    pivot_block = broadcast_whole(top_rows[:PB], owner_index, "grp")
    window_rows = broadcast_whole(top_rows[PB:], owner_index, "grp")
    symmetric = 0.5 * (pivot_block + pivot_block.T)
    pivot_factor, factor_inverse = factor_and_inverse(symmetric)
    solved = jnp.dot(panel_part, factor_inverse.T, precision=FAST)
    window = jnp.dot(window_rows, factor_inverse.T, precision=FAST)
    schur_part = local_rows[:, PB:] - jnp.dot(solved, window.T, precision=FAST)
    schur_part = add_rows(schur_part, 0, win_cols, flat_rows, trailing_rows.reshape(-1, win_cols))
    panel_rows = put_head(solved, pivot_factor, is_owner.astype(jnp.int32).reshape(1))
    return (panel_rows[None], schur_part[None])


def solution(mesh):
    placed = (
        P("front", "grp", None),
        P("front", "grp", None, None, None),
        P("front", "grp", None, None),
        P("front", "grp", None, None),
        P("front"),
    )
    return jax.shard_map(
        local,
        mesh=mesh,
        in_specs=placed,
        out_specs=(P("front", "grp", None), P("front", "grp", None)),
        check_vma=False,
    )
```

```python
import functools

import jax
import jax.numpy as jnp
from jax import lax
from jax.experimental import pallas as pl
from jax.experimental.pallas import tpu as pltpu
from jax.sharding import PartitionSpec as P

PB = 512
CAP = 2
BLK = 128
EXACT = lax.Precision.HIGHEST
FAST = lax.Precision.HIGH


def pack_slots(values, slot_index, front_count):
    empty = jnp.zeros((front_count * CAP,) + values.shape[1:], values.dtype)
    filled = empty.at[slot_index].set(values)
    return filled.reshape((front_count, CAP) + values.shape[1:])


def pairs(size, bit):
    return [(d, d ^ bit) for d in range(size)]


def broadcast_from(x, owner, axis):
    size = lax.axis_size(axis)
    me = lax.axis_index(axis)
    got = lax.ppermute(x, axis, pairs(size, 1))
    x = jnp.where(me == owner, x, got)
    half_rows = x.shape[0] // 2
    core = me % 2
    half = jnp.where(core == 0, x[:half_rows], x[half_rows:])
    bit = 2
    while bit < size:
        got = lax.ppermute(half, axis, pairs(size, bit))
        half = jnp.where(me // bit == owner // bit, half, got)
        bit *= 2
    other = lax.ppermute(half, axis, pairs(size, 1))
    return jnp.where(
        core == 0,
        jnp.concatenate([half, other], axis=0),
        jnp.concatenate([other, half], axis=0),
    )


def broadcast_whole(x, owner, axis):
    size = lax.axis_size(axis)
    me = lax.axis_index(axis)
    bit = 1
    while bit < size:
        got = lax.ppermute(x, axis, pairs(size, bit))
        x = jnp.where(me // bit == owner // bit, x, got)
        bit *= 2
    return x


def _mm(a, b):
    return jnp.dot(a, b, precision=EXACT, preferred_element_type=jnp.float32)


def _mm_t(a, b):
    return lax.dot_general(a, b, (((1,), (1,)), ((), ())), precision=EXACT, preferred_element_type=jnp.float32)


def _factor_kernel(s_ref, l_ref, inv_ref, w_ref, d_ref, dt_ref, di_ref):
    n = s_ref.shape[0]
    nb = n // BLK
    w_ref[...] = s_ref[...]
    l_ref[...] = jnp.zeros_like(l_ref)
    inv_ref[...] = jnp.zeros_like(inv_ref)
    sub = lax.broadcasted_iota(jnp.int32, (BLK, BLK), 0)
    lane = lax.broadcasted_iota(jnp.int32, (BLK, BLK), 1)
    lane1 = lax.broadcasted_iota(jnp.int32, (1, BLK), 1)
    sub1 = lax.broadcasted_iota(jnp.int32, (BLK, 1), 0)
    eye = jnp.where(sub == lane, 1.0, 0.0).astype(jnp.float32)

    def step(t, carry):
        j = 2 * t
        r0 = d_ref[pl.ds(j, 1), :]
        r1 = d_ref[pl.ds(j + 1, 1), :]
        d0 = jnp.sum(jnp.where(lane1 == j, r0, 0.0), axis=1, keepdims=True)
        e = jnp.sum(jnp.where(lane1 == j, r1, 0.0), axis=1, keepdims=True)
        d1 = jnp.sum(jnp.where(lane1 == j + 1, r1, 0.0), axis=1, keepdims=True)
        s0 = lax.rsqrt(d0)
        l10 = e * s0
        s1 = lax.rsqrt(d1 - l10 * l10)
        c0 = jnp.where(lane1 >= j, r0 * s0, 0.0)
        c1 = jnp.where(lane1 >= j + 1, (r1 - l10 * c0) * s1, 0.0)
        wv = d_ref[...]
        col0 = jnp.sum(jnp.where(lane == j, wv, 0.0), axis=1, keepdims=True)
        col1 = jnp.sum(jnp.where(lane == j + 1, wv, 0.0), axis=1, keepdims=True)
        ccol0 = jnp.where(sub1 >= j, col0 * s0, 0.0)
        ccol1 = jnp.where(sub1 >= j + 1, (col1 - l10 * ccol0) * s1, 0.0)
        d_ref[...] = wv - ccol0 * c0 - ccol1 * c1
        dt_ref[pl.ds(j, 1), :] = c0
        dt_ref[pl.ds(j + 1, 1), :] = c1
        x0 = di_ref[pl.ds(j, 1), :] * s0
        x1 = (di_ref[pl.ds(j + 1, 1), :] - l10 * x0) * s1
        below = sub1 > j + 1
        di_ref[...] = di_ref[...] - jnp.where(below, ccol0, 0.0) * x0 - jnp.where(below, ccol1, 0.0) * x1
        di_ref[pl.ds(j, 1), :] = x0
        di_ref[pl.ds(j + 1, 1), :] = x1
        return carry

    inv_diag = []
    for k in range(nb):
        lo, hi = k * BLK, (k + 1) * BLK
        d_ref[...] = w_ref[lo:hi, lo:hi]
        di_ref[...] = eye
        lax.fori_loop(0, BLK // 2, step, 0)
        lkk = dt_ref[...].T
        ikk = di_ref[...]
        l_ref[lo:hi, lo:hi] = lkk
        inv_ref[lo:hi, lo:hi] = ikk
        inv_diag.append(ikk)
        if k + 1 < nb:
            panel = _mm_t(w_ref[hi:, lo:hi], ikk)
            l_ref[hi:, lo:hi] = panel
            w_ref[hi:, hi:] = w_ref[hi:, hi:] - _mm_t(panel, panel)
    for i in range(nb):
        for j in range(i - 1, -1, -1):
            acc = _mm(l_ref[i * BLK:(i + 1) * BLK, j * BLK:i * BLK], inv_ref[j * BLK:i * BLK, j * BLK:(j + 1) * BLK])
            inv_ref[i * BLK:(i + 1) * BLK, j * BLK:(j + 1) * BLK] = -_mm(inv_diag[i], acc)


def factor_and_inverse(sym):
    n = sym.shape[0]
    return pl.pallas_call(
        _factor_kernel,
        out_shape=(jax.ShapeDtypeStruct((n, n), jnp.float32), jax.ShapeDtypeStruct((n, n), jnp.float32)),
        in_specs=[pl.BlockSpec(memory_space=pltpu.VMEM)],
        out_specs=(pl.BlockSpec(memory_space=pltpu.VMEM), pl.BlockSpec(memory_space=pltpu.VMEM)),
        scratch_shapes=[pltpu.VMEM((n, n), jnp.float32)] + [pltpu.VMEM((BLK, BLK), jnp.float32)] * 3,
    )(sym)


def _block_add_kernel(col0, idx_ref, base_ref, add_ref, out_ref, sem):
    width = out_ref.shape[1]
    copy = pltpu.make_async_copy(base_ref.at[:, pl.ds(col0, width)], out_ref, sem)
    copy.start()
    copy.wait()

    def accumulate(i, c):
        r = idx_ref[i]
        out_ref[pl.ds(r, 1), :] = out_ref[pl.ds(r, 1), :] + add_ref[pl.ds(i, 1), :]
        return c

    lax.fori_loop(0, add_ref.shape[0], accumulate, 0, unroll=8)


def add_rows(base, col0, width, rows, values):
    return pl.pallas_call(
        functools.partial(_block_add_kernel, col0),
        out_shape=jax.ShapeDtypeStruct((base.shape[0], width), base.dtype),
        in_specs=[
            pl.BlockSpec(memory_space=pltpu.SMEM),
            pl.BlockSpec(memory_space=pl.ANY),
            pl.BlockSpec(memory_space=pltpu.VMEM),
        ],
        out_specs=pl.BlockSpec(memory_space=pltpu.VMEM),
        scratch_shapes=[pltpu.SemaphoreType.DMA(())],
    )(rows, base, values)


def _head_kernel(flag_ref, factor_ref, solved_ref, out_ref, sem):
    @pl.when(flag_ref[0] == 1)
    def _():
        copy = pltpu.make_async_copy(factor_ref, out_ref.at[pl.ds(0, factor_ref.shape[0])], sem)
        copy.start()
        copy.wait()


def put_head(solved, factor, flag):
    return pl.pallas_call(
        _head_kernel,
        out_shape=jax.ShapeDtypeStruct(solved.shape, solved.dtype),
        in_specs=[
            pl.BlockSpec(memory_space=pltpu.SMEM),
            pl.BlockSpec(memory_space=pltpu.VMEM),
            pl.BlockSpec(memory_space=pl.ANY),
        ],
        out_specs=pl.BlockSpec(memory_space=pl.ANY),
        scratch_shapes=[pltpu.SemaphoreType.DMA(())],
        input_output_aliases={2: 0},
    )(flag, factor, solved)


def local(front_block, child_blocks, child_rows, child_dest, panel_owner):
    local_rows = front_block[0]
    front_count = lax.axis_size("front")
    blocks = child_blocks[0, 0]
    row_lists = child_rows[0, 0]
    target_front = child_dest[0, 0, :, 0]
    block_count = target_front.shape[0]
    position = jnp.arange(block_count, dtype=jnp.int32)
    same_front = target_front[:, None] == target_front[None, :]
    earlier = position[None, :] < position[:, None]
    slot_index = target_front * CAP + jnp.sum((same_front & earlier).astype(jnp.int32), axis=1)
    row_lanes = jnp.zeros(blocks.shape[:2] + (128,), jnp.float32).at[:, :, 0].set(row_lists.astype(jnp.float32))
    send_panel = pack_slots(jnp.concatenate([blocks[:, :, :PB], row_lanes], axis=2), slot_index, front_count)
    got_both = lax.all_to_all(send_panel, "front", split_axis=0, concat_axis=0, tiled=True)
    got_panel = got_both[..., :PB]
    flat_rows = got_both[..., PB].reshape(-1).astype(jnp.int32)
    panel_part = add_rows(local_rows, 0, PB, flat_rows, got_panel.reshape(-1, PB))
    send_trail = pack_slots(blocks[:, :, PB:], slot_index, front_count)
    trailing_rows = lax.all_to_all(send_trail, "front", split_axis=0, concat_axis=0, tiled=True)
    win_cols = local_rows.shape[1] - PB
    owner_index = panel_owner[0]
    is_owner = lax.axis_index("grp") == owner_index

    pivot_block = broadcast_from(panel_part[:PB], owner_index, "grp")
    window_rows = broadcast_whole(panel_part[PB:PB + win_cols], owner_index, "grp")
    symmetric = 0.5 * (pivot_block + pivot_block.T)
    pivot_factor, factor_inverse = factor_and_inverse(symmetric)
    solved = jnp.dot(panel_part, factor_inverse.T, precision=FAST)
    window = jnp.dot(window_rows, factor_inverse.T, precision=FAST)
    schur_part = local_rows[:, PB:] - jnp.dot(solved, window.T, precision=FAST)
    schur_part = add_rows(schur_part, 0, win_cols, flat_rows, trailing_rows.reshape(-1, win_cols))
    panel_rows = put_head(solved, pivot_factor, is_owner.astype(jnp.int32).reshape(1))
    return (panel_rows[None], schur_part[None])


def solution(mesh):
    placed = (
        P("front", "grp", None),
        P("front", "grp", None, None, None),
        P("front", "grp", None, None),
        P("front", "grp", None, None),
        P("front"),
    )
    return jax.shard_map(
        local,
        mesh=mesh,
        in_specs=placed,
        out_specs=(P("front", "grp", None), P("front", "grp", None)),
        check_vma=False,
    )
```

```python
import functools

import jax
import jax.numpy as jnp
from jax import lax
from jax.experimental import pallas as pl
from jax.experimental.pallas import tpu as pltpu
from jax.sharding import PartitionSpec as P

PB = 512
CAP = 2
BLK = 128
PARTS = 4
EXACT = lax.Precision.HIGHEST
FAST = lax.Precision.HIGH


def pack_slots(values, slot_index, front_count):
    empty = jnp.zeros((front_count * CAP,) + values.shape[1:], values.dtype)
    filled = empty.at[slot_index].set(values)
    return filled.reshape((front_count, CAP) + values.shape[1:])


def pairs(size, bit):
    return [(d, d ^ bit) for d in range(size)]


def broadcast_from(x, owner, axis):
    size = lax.axis_size(axis)
    me = lax.axis_index(axis)
    got = lax.ppermute(x, axis, pairs(size, 1))
    x = jnp.where(me == owner, x, got)
    half_rows = x.shape[0] // 2
    core = me % 2
    half = jnp.where(core == 0, x[:half_rows], x[half_rows:])
    bit = 2
    while bit < size:
        got = lax.ppermute(half, axis, pairs(size, bit))
        half = jnp.where(me // bit == owner // bit, half, got)
        bit *= 2
    other = lax.ppermute(half, axis, pairs(size, 1))
    return jnp.where(
        core == 0,
        jnp.concatenate([half, other], axis=0),
        jnp.concatenate([other, half], axis=0),
    )


def broadcast_whole(x, owner, axis):
    size = lax.axis_size(axis)
    me = lax.axis_index(axis)
    bit = 1
    while bit < size:
        got = lax.ppermute(x, axis, pairs(size, bit))
        x = jnp.where(me // bit == owner // bit, x, got)
        bit *= 2
    return x


def _mm(a, b):
    return jnp.dot(a, b, precision=EXACT, preferred_element_type=jnp.float32)


def _mm_t(a, b):
    return lax.dot_general(a, b, (((1,), (1,)), ((), ())), precision=EXACT, preferred_element_type=jnp.float32)


def _factor_kernel(s_ref, l_ref, inv_ref, w_ref, d_ref, dt_ref, di_ref):
    n = s_ref.shape[0]
    nb = n // BLK
    w_ref[...] = s_ref[...]
    l_ref[...] = jnp.zeros_like(l_ref)
    inv_ref[...] = jnp.zeros_like(inv_ref)
    sub = lax.broadcasted_iota(jnp.int32, (BLK, BLK), 0)
    lane = lax.broadcasted_iota(jnp.int32, (BLK, BLK), 1)
    lane1 = lax.broadcasted_iota(jnp.int32, (1, BLK), 1)
    sub1 = lax.broadcasted_iota(jnp.int32, (BLK, 1), 0)
    eye = jnp.where(sub == lane, 1.0, 0.0).astype(jnp.float32)

    def step(t, carry):
        j = 2 * t
        r0 = d_ref[pl.ds(j, 1), :]
        r1 = d_ref[pl.ds(j + 1, 1), :]
        d0 = jnp.sum(jnp.where(lane1 == j, r0, 0.0), axis=1, keepdims=True)
        e = jnp.sum(jnp.where(lane1 == j, r1, 0.0), axis=1, keepdims=True)
        d1 = jnp.sum(jnp.where(lane1 == j + 1, r1, 0.0), axis=1, keepdims=True)
        s0 = lax.rsqrt(d0)
        l10 = e * s0
        s1 = lax.rsqrt(d1 - l10 * l10)
        c0 = jnp.where(lane1 >= j, r0 * s0, 0.0)
        c1 = jnp.where(lane1 >= j + 1, (r1 - l10 * c0) * s1, 0.0)
        wv = d_ref[...]
        col0 = jnp.sum(jnp.where(lane == j, wv, 0.0), axis=1, keepdims=True)
        col1 = jnp.sum(jnp.where(lane == j + 1, wv, 0.0), axis=1, keepdims=True)
        ccol0 = jnp.where(sub1 >= j, col0 * s0, 0.0)
        ccol1 = jnp.where(sub1 >= j + 1, (col1 - l10 * ccol0) * s1, 0.0)
        d_ref[...] = wv - ccol0 * c0 - ccol1 * c1
        dt_ref[pl.ds(j, 1), :] = c0
        dt_ref[pl.ds(j + 1, 1), :] = c1
        x0 = di_ref[pl.ds(j, 1), :] * s0
        x1 = (di_ref[pl.ds(j + 1, 1), :] - l10 * x0) * s1
        below = sub1 > j + 1
        di_ref[...] = di_ref[...] - jnp.where(below, ccol0, 0.0) * x0 - jnp.where(below, ccol1, 0.0) * x1
        di_ref[pl.ds(j, 1), :] = x0
        di_ref[pl.ds(j + 1, 1), :] = x1
        return carry

    inv_diag = []
    for k in range(nb):
        lo, hi = k * BLK, (k + 1) * BLK
        d_ref[...] = w_ref[lo:hi, lo:hi]
        di_ref[...] = eye
        lax.fori_loop(0, BLK // 2, step, 0)
        lkk = dt_ref[...].T
        ikk = di_ref[...]
        l_ref[lo:hi, lo:hi] = lkk
        inv_ref[lo:hi, lo:hi] = ikk
        inv_diag.append(ikk)
        if k + 1 < nb:
            panel = _mm_t(w_ref[hi:, lo:hi], ikk)
            l_ref[hi:, lo:hi] = panel
            w_ref[hi:, hi:] = w_ref[hi:, hi:] - _mm_t(panel, panel)
    for i in range(nb):
        for j in range(i - 1, -1, -1):
            acc = _mm(l_ref[i * BLK:(i + 1) * BLK, j * BLK:i * BLK], inv_ref[j * BLK:i * BLK, j * BLK:(j + 1) * BLK])
            inv_ref[i * BLK:(i + 1) * BLK, j * BLK:(j + 1) * BLK] = -_mm(inv_diag[i], acc)


def factor_and_inverse(sym):
    n = sym.shape[0]
    return pl.pallas_call(
        _factor_kernel,
        out_shape=(jax.ShapeDtypeStruct((n, n), jnp.float32), jax.ShapeDtypeStruct((n, n), jnp.float32)),
        in_specs=[pl.BlockSpec(memory_space=pltpu.VMEM)],
        out_specs=(pl.BlockSpec(memory_space=pltpu.VMEM), pl.BlockSpec(memory_space=pltpu.VMEM)),
        scratch_shapes=[pltpu.VMEM((n, n), jnp.float32)] + [pltpu.VMEM((BLK, BLK), jnp.float32)] * 3,
    )(sym)


def _block_add_kernel(col0, idx_ref, base_ref, add_ref, out_ref, sems):
    rows, width = out_ref.shape
    part = rows // PARTS
    copies = [
        pltpu.make_async_copy(
            base_ref.at[pl.ds(p * part, part), pl.ds(col0, width)], out_ref.at[pl.ds(p * part, part)], sems.at[p]
        )
        for p in range(PARTS)
    ]
    for copy in copies:
        copy.start()
    for copy in copies:
        copy.wait()

    def accumulate(i, c):
        r = idx_ref[i]
        out_ref[pl.ds(r, 1), :] = out_ref[pl.ds(r, 1), :] + add_ref[pl.ds(i, 1), :]
        return c

    lax.fori_loop(0, add_ref.shape[0], accumulate, 0, unroll=8)


def add_rows(base, col0, width, rows, values):
    return pl.pallas_call(
        functools.partial(_block_add_kernel, col0),
        out_shape=jax.ShapeDtypeStruct((base.shape[0], width), base.dtype),
        in_specs=[
            pl.BlockSpec(memory_space=pltpu.SMEM),
            pl.BlockSpec(memory_space=pl.ANY),
            pl.BlockSpec(memory_space=pltpu.VMEM),
        ],
        out_specs=pl.BlockSpec(memory_space=pltpu.VMEM),
        scratch_shapes=[pltpu.SemaphoreType.DMA((PARTS,))],
    )(rows, base, values)


def _head_kernel(flag_ref, factor_ref, solved_ref, out_ref, sem):
    @pl.when(flag_ref[0] == 1)
    def _():
        copy = pltpu.make_async_copy(factor_ref, out_ref.at[pl.ds(0, factor_ref.shape[0])], sem)
        copy.start()
        copy.wait()


def put_head(solved, factor, flag):
    return pl.pallas_call(
        _head_kernel,
        out_shape=jax.ShapeDtypeStruct(solved.shape, solved.dtype),
        in_specs=[
            pl.BlockSpec(memory_space=pltpu.SMEM),
            pl.BlockSpec(memory_space=pltpu.VMEM),
            pl.BlockSpec(memory_space=pl.ANY),
        ],
        out_specs=pl.BlockSpec(memory_space=pl.ANY),
        scratch_shapes=[pltpu.SemaphoreType.DMA(())],
        input_output_aliases={2: 0},
    )(flag, factor, solved)


def local(front_block, child_blocks, child_rows, child_dest, panel_owner):
    local_rows = front_block[0]
    front_count = lax.axis_size("front")
    blocks = child_blocks[0, 0]
    row_lists = child_rows[0, 0]
    target_front = child_dest[0, 0, :, 0]
    block_count = target_front.shape[0]
    position = jnp.arange(block_count, dtype=jnp.int32)
    same_front = target_front[:, None] == target_front[None, :]
    earlier = position[None, :] < position[:, None]
    slot_index = target_front * CAP + jnp.sum((same_front & earlier).astype(jnp.int32), axis=1)
    row_lanes = jnp.zeros(blocks.shape[:2] + (128,), jnp.float32).at[:, :, 0].set(row_lists.astype(jnp.float32))
    send_panel = pack_slots(jnp.concatenate([blocks[:, :, :PB], row_lanes], axis=2), slot_index, front_count)
    got_both = lax.all_to_all(send_panel, "front", split_axis=0, concat_axis=0, tiled=True)
    got_panel = got_both[..., :PB]
    flat_rows = got_both[..., PB].reshape(-1).astype(jnp.int32)
    panel_part = add_rows(local_rows, 0, PB, flat_rows, got_panel.reshape(-1, PB))
    send_trail = pack_slots(blocks[:, :, PB:], slot_index, front_count)
    trailing_rows = lax.all_to_all(send_trail, "front", split_axis=0, concat_axis=0, tiled=True)
    win_cols = local_rows.shape[1] - PB
    owner_index = panel_owner[0]
    is_owner = lax.axis_index("grp") == owner_index

    pivot_block = broadcast_from(panel_part[:PB], owner_index, "grp")
    window_rows = broadcast_whole(panel_part[PB:PB + win_cols], owner_index, "grp")
    symmetric = 0.5 * (pivot_block + pivot_block.T)
    pivot_factor, factor_inverse = factor_and_inverse(symmetric)
    solved = jnp.dot(panel_part, factor_inverse.T, precision=FAST)
    window = jnp.dot(window_rows, factor_inverse.T, precision=FAST)
    schur_part = local_rows[:, PB:] - jnp.dot(solved, window.T, precision=FAST)
    schur_part = add_rows(schur_part, 0, win_cols, flat_rows, trailing_rows.reshape(-1, win_cols))
    panel_rows = put_head(solved, pivot_factor, is_owner.astype(jnp.int32).reshape(1))
    return (panel_rows[None], schur_part[None])


def solution(mesh):
    placed = (
        P("front", "grp", None),
        P("front", "grp", None, None, None),
        P("front", "grp", None, None),
        P("front", "grp", None, None),
        P("front"),
    )
    return jax.shard_map(
        local,
        mesh=mesh,
        in_specs=placed,
        out_specs=(P("front", "grp", None), P("front", "grp", None)),
        check_vma=False,
    )
```

```python
import functools

import jax
import jax.numpy as jnp
from jax import lax
from jax.experimental import pallas as pl
from jax.experimental.pallas import tpu as pltpu
from jax.sharding import PartitionSpec as P

PB = 512
CAP = 2
BLK = 128
EXACT = lax.Precision.HIGHEST
FAST = lax.Precision.HIGH


def pack_slots(values, slot_index, front_count):
    empty = jnp.zeros((front_count * CAP,) + values.shape[1:], values.dtype)
    filled = empty.at[slot_index].set(values)
    return filled.reshape((front_count, CAP) + values.shape[1:])


def pairs(size, bit):
    return [(d, d ^ bit) for d in range(size)]


def broadcast_from(x, owner, axis):
    size = lax.axis_size(axis)
    me = lax.axis_index(axis)
    got = lax.ppermute(x, axis, pairs(size, 1))
    x = jnp.where(me == owner, x, got)
    half_rows = x.shape[0] // 2
    core = me % 2
    half = jnp.where(core == 0, x[:half_rows], x[half_rows:])
    bit = 2
    while bit < size:
        got = lax.ppermute(half, axis, pairs(size, bit))
        half = jnp.where(me // bit == owner // bit, half, got)
        bit *= 2
    other = lax.ppermute(half, axis, pairs(size, 1))
    return jnp.where(
        core == 0,
        jnp.concatenate([half, other], axis=0),
        jnp.concatenate([other, half], axis=0),
    )


def broadcast_whole(x, owner, axis):
    size = lax.axis_size(axis)
    me = lax.axis_index(axis)
    bit = 1
    while bit < size:
        got = lax.ppermute(x, axis, pairs(size, bit))
        x = jnp.where(me // bit == owner // bit, x, got)
        bit *= 2
    return x


def _mm(a, b):
    return jnp.dot(a, b, precision=EXACT, preferred_element_type=jnp.float32)


def _mm_t(a, b):
    return lax.dot_general(a, b, (((1,), (1,)), ((), ())), precision=EXACT, preferred_element_type=jnp.float32)


def _factor_kernel(s_ref, l_ref, inv_ref, w_ref, d_ref, dt_ref, di_ref):
    n = s_ref.shape[0]
    nb = n // BLK
    pivot = s_ref[...]
    w_ref[...] = 0.5 * (pivot + pivot.T)
    l_ref[...] = jnp.zeros_like(l_ref)
    inv_ref[...] = jnp.zeros_like(inv_ref)
    sub = lax.broadcasted_iota(jnp.int32, (BLK, BLK), 0)
    lane = lax.broadcasted_iota(jnp.int32, (BLK, BLK), 1)
    lane1 = lax.broadcasted_iota(jnp.int32, (1, BLK), 1)
    sub1 = lax.broadcasted_iota(jnp.int32, (BLK, 1), 0)
    eye = jnp.where(sub == lane, 1.0, 0.0).astype(jnp.float32)

    def step(t, carry):
        j = 2 * t
        r0 = d_ref[pl.ds(j, 1), :]
        r1 = d_ref[pl.ds(j + 1, 1), :]
        d0 = jnp.sum(jnp.where(lane1 == j, r0, 0.0), axis=1, keepdims=True)
        e = jnp.sum(jnp.where(lane1 == j, r1, 0.0), axis=1, keepdims=True)
        d1 = jnp.sum(jnp.where(lane1 == j + 1, r1, 0.0), axis=1, keepdims=True)
        s0 = lax.rsqrt(d0)
        l10 = e * s0
        s1 = lax.rsqrt(d1 - l10 * l10)
        c0 = jnp.where(lane1 >= j, r0 * s0, 0.0)
        c1 = jnp.where(lane1 >= j + 1, (r1 - l10 * c0) * s1, 0.0)
        wv = d_ref[...]
        col0 = jnp.sum(jnp.where(lane == j, wv, 0.0), axis=1, keepdims=True)
        col1 = jnp.sum(jnp.where(lane == j + 1, wv, 0.0), axis=1, keepdims=True)
        ccol0 = jnp.where(sub1 >= j, col0 * s0, 0.0)
        ccol1 = jnp.where(sub1 >= j + 1, (col1 - l10 * ccol0) * s1, 0.0)
        d_ref[...] = wv - ccol0 * c0 - ccol1 * c1
        dt_ref[pl.ds(j, 1), :] = c0
        dt_ref[pl.ds(j + 1, 1), :] = c1
        x0 = di_ref[pl.ds(j, 1), :] * s0
        x1 = (di_ref[pl.ds(j + 1, 1), :] - l10 * x0) * s1
        below = sub1 > j + 1
        di_ref[...] = di_ref[...] - jnp.where(below, ccol0, 0.0) * x0 - jnp.where(below, ccol1, 0.0) * x1
        di_ref[pl.ds(j, 1), :] = x0
        di_ref[pl.ds(j + 1, 1), :] = x1
        return carry

    inv_diag = []
    for k in range(nb):
        lo, hi = k * BLK, (k + 1) * BLK
        d_ref[...] = w_ref[lo:hi, lo:hi]
        di_ref[...] = eye
        lax.fori_loop(0, BLK // 2, step, 0)
        lkk = dt_ref[...].T
        ikk = di_ref[...]
        l_ref[lo:hi, lo:hi] = lkk
        inv_ref[lo:hi, lo:hi] = ikk
        inv_diag.append(ikk)
        if k + 1 < nb:
            panel = _mm_t(w_ref[hi:, lo:hi], ikk)
            l_ref[hi:, lo:hi] = panel
            w_ref[hi:, hi:] = w_ref[hi:, hi:] - _mm_t(panel, panel)
    for i in range(nb):
        for j in range(i - 1, -1, -1):
            acc = _mm(l_ref[i * BLK:(i + 1) * BLK, j * BLK:i * BLK], inv_ref[j * BLK:i * BLK, j * BLK:(j + 1) * BLK])
            inv_ref[i * BLK:(i + 1) * BLK, j * BLK:(j + 1) * BLK] = -_mm(inv_diag[i], acc)


def factor_and_inverse(sym):
    n = sym.shape[0]
    return pl.pallas_call(
        _factor_kernel,
        out_shape=(jax.ShapeDtypeStruct((n, n), jnp.float32), jax.ShapeDtypeStruct((n, n), jnp.float32)),
        in_specs=[pl.BlockSpec(memory_space=pltpu.VMEM)],
        out_specs=(pl.BlockSpec(memory_space=pltpu.VMEM), pl.BlockSpec(memory_space=pltpu.VMEM)),
        scratch_shapes=[pltpu.VMEM((n, n), jnp.float32)] + [pltpu.VMEM((BLK, BLK), jnp.float32)] * 3,
    )(sym)


def _block_add_kernel(col0, idx_ref, base_ref, add_ref, out_ref, sem):
    width = out_ref.shape[1]
    copy = pltpu.make_async_copy(base_ref.at[:, pl.ds(col0, width)], out_ref, sem)
    copy.start()
    copy.wait()

    def accumulate(i, c):
        r = idx_ref[i]
        out_ref[pl.ds(r, 1), :] = out_ref[pl.ds(r, 1), :] + add_ref[pl.ds(i, 1), :]
        return c

    lax.fori_loop(0, add_ref.shape[0], accumulate, 0, unroll=8)


def add_rows(base, col0, width, rows, values):
    return pl.pallas_call(
        functools.partial(_block_add_kernel, col0),
        out_shape=jax.ShapeDtypeStruct((base.shape[0], width), base.dtype),
        in_specs=[
            pl.BlockSpec(memory_space=pltpu.SMEM),
            pl.BlockSpec(memory_space=pl.ANY),
            pl.BlockSpec(memory_space=pltpu.VMEM),
        ],
        out_specs=pl.BlockSpec(memory_space=pltpu.VMEM),
        scratch_shapes=[pltpu.SemaphoreType.DMA(())],
    )(rows, base, values)


def _head_kernel(flag_ref, factor_ref, solved_ref, out_ref, sem):
    @pl.when(flag_ref[0] == 1)
    def _():
        copy = pltpu.make_async_copy(factor_ref, out_ref.at[pl.ds(0, factor_ref.shape[0])], sem)
        copy.start()
        copy.wait()


def put_head(solved, factor, flag):
    return pl.pallas_call(
        _head_kernel,
        out_shape=jax.ShapeDtypeStruct(solved.shape, solved.dtype),
        in_specs=[
            pl.BlockSpec(memory_space=pltpu.SMEM),
            pl.BlockSpec(memory_space=pltpu.VMEM),
            pl.BlockSpec(memory_space=pl.ANY),
        ],
        out_specs=pl.BlockSpec(memory_space=pl.ANY),
        scratch_shapes=[pltpu.SemaphoreType.DMA(())],
        input_output_aliases={2: 0},
    )(flag, factor, solved)


def local(front_block, child_blocks, child_rows, child_dest, panel_owner):
    local_rows = front_block[0]
    front_count = lax.axis_size("front")
    blocks = child_blocks[0, 0]
    row_lists = child_rows[0, 0]
    target_front = child_dest[0, 0, :, 0]
    block_count = target_front.shape[0]
    position = jnp.arange(block_count, dtype=jnp.int32)
    same_front = target_front[:, None] == target_front[None, :]
    earlier = position[None, :] < position[:, None]
    slot_index = target_front * CAP + jnp.sum((same_front & earlier).astype(jnp.int32), axis=1)
    row_lanes = jnp.zeros(blocks.shape[:2] + (128,), jnp.float32).at[:, :, 0].set(row_lists.astype(jnp.float32))
    send_panel = pack_slots(jnp.concatenate([blocks[:, :, :PB], row_lanes], axis=2), slot_index, front_count)
    got_both = lax.all_to_all(send_panel, "front", split_axis=0, concat_axis=0, tiled=True)
    got_panel = got_both[..., :PB]
    flat_rows = got_both[..., PB].reshape(-1).astype(jnp.int32)
    panel_part = add_rows(local_rows, 0, PB, flat_rows, got_panel.reshape(-1, PB))
    send_trail = pack_slots(blocks[:, :, PB:], slot_index, front_count)
    trailing_rows = lax.all_to_all(send_trail, "front", split_axis=0, concat_axis=0, tiled=True)
    win_cols = local_rows.shape[1] - PB
    owner_index = panel_owner[0]
    is_owner = lax.axis_index("grp") == owner_index

    pivot_block = broadcast_from(panel_part[:PB], owner_index, "grp")
    window_rows = broadcast_whole(panel_part[PB:PB + win_cols], owner_index, "grp")
    pivot_factor, factor_inverse = factor_and_inverse(pivot_block)
    solved = jnp.dot(panel_part, factor_inverse.T, precision=FAST)
    window = jnp.dot(window_rows, factor_inverse.T, precision=FAST)
    schur_part = local_rows[:, PB:] - jnp.dot(solved, window.T, precision=FAST)
    schur_part = add_rows(schur_part, 0, win_cols, flat_rows, trailing_rows.reshape(-1, win_cols))
    panel_rows = put_head(solved, pivot_factor, is_owner.astype(jnp.int32).reshape(1))
    return (panel_rows[None], schur_part[None])


def solution(mesh):
    placed = (
        P("front", "grp", None),
        P("front", "grp", None, None, None),
        P("front", "grp", None, None),
        P("front", "grp", None, None),
        P("front"),
    )
    return jax.shard_map(
        local,
        mesh=mesh,
        in_specs=placed,
        out_specs=(P("front", "grp", None), P("front", "grp", None)),
        check_vma=False,
    )
```

```python
import functools

import jax
import jax.numpy as jnp
from jax import lax
from jax.experimental import pallas as pl
from jax.experimental.pallas import tpu as pltpu
from jax.sharding import PartitionSpec as P

PB = 512
CAP = 2
BLK = 128
EXACT = lax.Precision.HIGHEST
FAST = lax.Precision.HIGH


def pack_slots(values, slot_index, front_count):
    empty = jnp.zeros((front_count * CAP,) + values.shape[1:], values.dtype)
    filled = empty.at[slot_index].set(values)
    return filled.reshape((front_count, CAP) + values.shape[1:])


def pairs(size, bit):
    return [(d, d ^ bit) for d in range(size)]


def broadcast_from(x, owner, axis):
    size = lax.axis_size(axis)
    me = lax.axis_index(axis)
    got = lax.ppermute(x, axis, pairs(size, 1))
    x = jnp.where(me == owner, x, got)
    half_rows = x.shape[0] // 2
    core = me % 2
    half = jnp.where(core == 0, x[:half_rows], x[half_rows:])
    bit = 2
    while bit < size:
        got = lax.ppermute(half, axis, pairs(size, bit))
        half = jnp.where(me // bit == owner // bit, half, got)
        bit *= 2
    other = lax.ppermute(half, axis, pairs(size, 1))
    return jnp.where(
        core == 0,
        jnp.concatenate([half, other], axis=0),
        jnp.concatenate([other, half], axis=0),
    )


def broadcast_halves(x, owner, axis):
    size = lax.axis_size(axis)
    me = lax.axis_index(axis)
    got = lax.ppermute(x, axis, pairs(size, 1))
    x = jnp.where(me == owner, x, got)
    half_rows = x.shape[0] // 2
    core = me % 2
    half = jnp.where(core == 0, x[:half_rows], x[half_rows:])
    bit = 2
    while bit < size:
        got = lax.ppermute(half, axis, pairs(size, bit))
        half = jnp.where(me // bit == owner // bit, half, got)
        bit *= 2
    other = lax.ppermute(half, axis, pairs(size, 1))
    return half, other, (core == 0).astype(jnp.int32).reshape(1)


def broadcast_whole(x, owner, axis):
    size = lax.axis_size(axis)
    me = lax.axis_index(axis)
    bit = 1
    while bit < size:
        got = lax.ppermute(x, axis, pairs(size, bit))
        x = jnp.where(me // bit == owner // bit, x, got)
        bit *= 2
    return x


def _mm(a, b):
    return jnp.dot(a, b, precision=EXACT, preferred_element_type=jnp.float32)


def _mm_t(a, b):
    return lax.dot_general(a, b, (((1,), (1,)), ((), ())), precision=EXACT, preferred_element_type=jnp.float32)


def _factor_kernel(first_ref, mine_ref, other_ref, l_ref, inv_ref, w_ref, d_ref, dt_ref, di_ref):
    n = l_ref.shape[0]
    nb = n // BLK
    first = first_ref[0] == 1
    mine = mine_ref[...]
    other = other_ref[...]
    pivot = jnp.concatenate([jnp.where(first, mine, other), jnp.where(first, other, mine)], axis=0)
    w_ref[...] = 0.5 * (pivot + pivot.T)
    l_ref[...] = jnp.zeros_like(l_ref)
    inv_ref[...] = jnp.zeros_like(inv_ref)
    sub = lax.broadcasted_iota(jnp.int32, (BLK, BLK), 0)
    lane = lax.broadcasted_iota(jnp.int32, (BLK, BLK), 1)
    lane1 = lax.broadcasted_iota(jnp.int32, (1, BLK), 1)
    sub1 = lax.broadcasted_iota(jnp.int32, (BLK, 1), 0)
    eye = jnp.where(sub == lane, 1.0, 0.0).astype(jnp.float32)

    def step(t, carry):
        j = 2 * t
        r0 = d_ref[pl.ds(j, 1), :]
        r1 = d_ref[pl.ds(j + 1, 1), :]
        d0 = jnp.sum(jnp.where(lane1 == j, r0, 0.0), axis=1, keepdims=True)
        e = jnp.sum(jnp.where(lane1 == j, r1, 0.0), axis=1, keepdims=True)
        d1 = jnp.sum(jnp.where(lane1 == j + 1, r1, 0.0), axis=1, keepdims=True)
        s0 = lax.rsqrt(d0)
        l10 = e * s0
        s1 = lax.rsqrt(d1 - l10 * l10)
        c0 = jnp.where(lane1 >= j, r0 * s0, 0.0)
        c1 = jnp.where(lane1 >= j + 1, (r1 - l10 * c0) * s1, 0.0)
        wv = d_ref[...]
        col0 = jnp.sum(jnp.where(lane == j, wv, 0.0), axis=1, keepdims=True)
        col1 = jnp.sum(jnp.where(lane == j + 1, wv, 0.0), axis=1, keepdims=True)
        ccol0 = jnp.where(sub1 >= j, col0 * s0, 0.0)
        ccol1 = jnp.where(sub1 >= j + 1, (col1 - l10 * ccol0) * s1, 0.0)
        d_ref[...] = wv - ccol0 * c0 - ccol1 * c1
        dt_ref[pl.ds(j, 1), :] = c0
        dt_ref[pl.ds(j + 1, 1), :] = c1
        x0 = di_ref[pl.ds(j, 1), :] * s0
        x1 = (di_ref[pl.ds(j + 1, 1), :] - l10 * x0) * s1
        below = sub1 > j + 1
        di_ref[...] = di_ref[...] - jnp.where(below, ccol0, 0.0) * x0 - jnp.where(below, ccol1, 0.0) * x1
        di_ref[pl.ds(j, 1), :] = x0
        di_ref[pl.ds(j + 1, 1), :] = x1
        return carry

    inv_diag = []
    for k in range(nb):
        lo, hi = k * BLK, (k + 1) * BLK
        d_ref[...] = w_ref[lo:hi, lo:hi]
        di_ref[...] = eye
        lax.fori_loop(0, BLK // 2, step, 0)
        lkk = dt_ref[...].T
        ikk = di_ref[...]
        l_ref[lo:hi, lo:hi] = lkk
        inv_ref[lo:hi, lo:hi] = ikk
        inv_diag.append(ikk)
        if k + 1 < nb:
            panel = _mm_t(w_ref[hi:, lo:hi], ikk)
            l_ref[hi:, lo:hi] = panel
            w_ref[hi:, hi:] = w_ref[hi:, hi:] - _mm_t(panel, panel)
    for i in range(nb):
        for j in range(i - 1, -1, -1):
            acc = _mm(l_ref[i * BLK:(i + 1) * BLK, j * BLK:i * BLK], inv_ref[j * BLK:i * BLK, j * BLK:(j + 1) * BLK])
            inv_ref[i * BLK:(i + 1) * BLK, j * BLK:(j + 1) * BLK] = -_mm(inv_diag[i], acc)


def factor_and_inverse(mine, other, first):
    n = mine.shape[1]
    return pl.pallas_call(
        _factor_kernel,
        out_shape=(jax.ShapeDtypeStruct((n, n), jnp.float32), jax.ShapeDtypeStruct((n, n), jnp.float32)),
        in_specs=[pl.BlockSpec(memory_space=pltpu.SMEM)] + [pl.BlockSpec(memory_space=pltpu.VMEM)] * 2,
        out_specs=(pl.BlockSpec(memory_space=pltpu.VMEM), pl.BlockSpec(memory_space=pltpu.VMEM)),
        scratch_shapes=[pltpu.VMEM((n, n), jnp.float32)] + [pltpu.VMEM((BLK, BLK), jnp.float32)] * 3,
    )(first, mine, other)


def _block_add_kernel(col0, idx_ref, base_ref, add_ref, out_ref, sem):
    width = out_ref.shape[1]
    copy = pltpu.make_async_copy(base_ref.at[:, pl.ds(col0, width)], out_ref, sem)
    copy.start()
    copy.wait()

    def accumulate(i, c):
        r = idx_ref[i]
        out_ref[pl.ds(r, 1), :] = out_ref[pl.ds(r, 1), :] + add_ref[pl.ds(i, 1), :]
        return c

    lax.fori_loop(0, add_ref.shape[0], accumulate, 0, unroll=8)


def add_rows(base, col0, width, rows, values):
    return pl.pallas_call(
        functools.partial(_block_add_kernel, col0),
        out_shape=jax.ShapeDtypeStruct((base.shape[0], width), base.dtype),
        in_specs=[
            pl.BlockSpec(memory_space=pltpu.SMEM),
            pl.BlockSpec(memory_space=pl.ANY),
            pl.BlockSpec(memory_space=pltpu.VMEM),
        ],
        out_specs=pl.BlockSpec(memory_space=pltpu.VMEM),
        scratch_shapes=[pltpu.SemaphoreType.DMA(())],
    )(rows, base, values)


def _head_kernel(flag_ref, factor_ref, solved_ref, out_ref, sem):
    @pl.when(flag_ref[0] == 1)
    def _():
        copy = pltpu.make_async_copy(factor_ref, out_ref.at[pl.ds(0, factor_ref.shape[0])], sem)
        copy.start()
        copy.wait()


def put_head(solved, factor, flag):
    return pl.pallas_call(
        _head_kernel,
        out_shape=jax.ShapeDtypeStruct(solved.shape, solved.dtype),
        in_specs=[
            pl.BlockSpec(memory_space=pltpu.SMEM),
            pl.BlockSpec(memory_space=pltpu.VMEM),
            pl.BlockSpec(memory_space=pl.ANY),
        ],
        out_specs=pl.BlockSpec(memory_space=pl.ANY),
        scratch_shapes=[pltpu.SemaphoreType.DMA(())],
        input_output_aliases={2: 0},
    )(flag, factor, solved)


def local(front_block, child_blocks, child_rows, child_dest, panel_owner):
    local_rows = front_block[0]
    front_count = lax.axis_size("front")
    blocks = child_blocks[0, 0]
    row_lists = child_rows[0, 0]
    target_front = child_dest[0, 0, :, 0]
    block_count = target_front.shape[0]
    position = jnp.arange(block_count, dtype=jnp.int32)
    same_front = target_front[:, None] == target_front[None, :]
    earlier = position[None, :] < position[:, None]
    slot_index = target_front * CAP + jnp.sum((same_front & earlier).astype(jnp.int32), axis=1)
    row_lanes = jnp.zeros(blocks.shape[:2] + (128,), jnp.float32).at[:, :, 0].set(row_lists.astype(jnp.float32))
    send_panel = pack_slots(jnp.concatenate([blocks[:, :, :PB], row_lanes], axis=2), slot_index, front_count)
    got_both = lax.all_to_all(send_panel, "front", split_axis=0, concat_axis=0, tiled=True)
    got_panel = got_both[..., :PB]
    flat_rows = got_both[..., PB].reshape(-1).astype(jnp.int32)
    panel_part = add_rows(local_rows, 0, PB, flat_rows, got_panel.reshape(-1, PB))
    send_trail = pack_slots(blocks[:, :, PB:], slot_index, front_count)
    trailing_rows = lax.all_to_all(send_trail, "front", split_axis=0, concat_axis=0, tiled=True)
    win_cols = local_rows.shape[1] - PB
    owner_index = panel_owner[0]
    is_owner = lax.axis_index("grp") == owner_index

    pivot_mine, pivot_other, pivot_first = broadcast_halves(panel_part[:PB], owner_index, "grp")
    window_rows = broadcast_whole(panel_part[PB:PB + win_cols], owner_index, "grp")
    pivot_factor, factor_inverse = factor_and_inverse(pivot_mine, pivot_other, pivot_first)
    solved = jnp.dot(panel_part, factor_inverse.T, precision=FAST)
    window = jnp.dot(window_rows, factor_inverse.T, precision=FAST)
    schur_part = local_rows[:, PB:] - jnp.dot(solved, window.T, precision=FAST)
    schur_part = add_rows(schur_part, 0, win_cols, flat_rows, trailing_rows.reshape(-1, win_cols))
    panel_rows = put_head(solved, pivot_factor, is_owner.astype(jnp.int32).reshape(1))
    return (panel_rows[None], schur_part[None])


def solution(mesh):
    placed = (
        P("front", "grp", None),
        P("front", "grp", None, None, None),
        P("front", "grp", None, None),
        P("front", "grp", None, None),
        P("front"),
    )
    return jax.shard_map(
        local,
        mesh=mesh,
        in_specs=placed,
        out_specs=(P("front", "grp", None), P("front", "grp", None)),
        check_vma=False,
    )
```
